32 devices in a mesh: groups: 2 (over y), ctx: 4 (over x, core), tp: 4 (over z).
Axes of the slice: x: 2, y: 2, z: 4, core: 2. Of those that a mesh axis runs over, the one named last changes fastest.
Arguments:
- question_hidden: bfloat16 [256, 8192], P(('groups', 'ctx')), parts along dimension 0, may hold values from -1800 to 1800
- recomp_hidden: bfloat16 [512, 8192], P(('groups', 'ctx')), parts along dimension 0, may hold values from -1800 to 1800
- norm_gain: bfloat16 [8192], replicated, may hold values from 0.099609375 to 1.8984375
- w_query: bfloat16 [8192, 8192], P('ctx', 'tp'), may hold values from -0.0625 to 0.0625
- w_keyval: bfloat16 [8192, 2, 1024], P('ctx', None, 'tp'), may hold values from -0.25 to 0.25
- pool_codes: bfloat16 [384, 2, 64, 1024], P(('groups', 'ctx'), None, None, 'tp'), parts along dimension 0, may hold values from -127 to 127
- pool_scales: bfloat16 [384, 2, 8], P(('groups', 'ctx'), None, 'tp'), parts along dimension 0, may hold values from 0.025 to 2
- block_owner: int32 [256, 1], P('groups'), parts along dimension 0, may hold values from 0 to 3; in each aligned block of 32 rows (0 to 31, 32 to 63, ...) at most 16 rows name the same one
- block_slot: int32 [256], P('groups'), parts along dimension 0, may hold values from 0 to 47
- recomp_pos: int32 [512], P('groups'), parts along dimension 0, may hold values from 0 to 8191, as said below
Outputs:
- attended: bfloat16 [256, 8192], P(('groups', 'ctx'), 'tp'), parts along dimension 0
- kv_cache: bfloat16 [2, 16384, 1024], P(None, ('groups', 'ctx'), 'tp'), parts along dimension 1
The draws below stay inside these ranges and needn't reach their ends.
There are 2 independent parts, one for each index of `groups`. The reference program is written for one: setup_inputs(seed, part) draws one part's arguments, and reference() takes and returns one part's arrays. A program takes and returns all parts, laid end to end along the dimension named above; an argument that names none is the same for every part. Nothing has to cross between parts.
Inputs may be any that keep to these rules, and one draw needn't show every extreme that they name: Among the 32 context blocks of each index of ctx (rows of block_owner in aligned blocks), at most 16 name the same pool shard. `recomp_pos`: 256 distinct positions in no particular order; the first and the last context position are always listed.
All inputs are finite; a program needn't handle non-finite values.
Results may differ from the reference program's by a relative error of at most 0.018.
The reference program's roundings to bfloat16 on the way (of `normed_question`, `normed_recomp`, `query`, `question_kv`, `recomp_kv`, `cached` and `weights_low`) count: a program that leaves them out, or rounds other values in their place, can miss the bound.
Values may be sent and summed in bfloat16 or wider, within the bound.
No kernel may reach another device: no remote copies, remote signals or barrier semaphores. Data moves between devices by JAX's collectives and lax.ppermute only.
A program may use at most 128 MiB of HBM per device.

```python
import math
import jax
import jax.numpy as jnp
import numpy as np
from jax import lax

D = 8192
NH = 64
KVH = 8
HD = 128
GROUP = 8
BLOCK = 64
POOL_DEV = 48
QTOK = 128
RECOMP = 256
CTX_TOK = 8192
BLK_DEV = 32
CTX_BLOCKS = 128
POOL_BLOCKS = 192
OWNERS = 4
MOST = 16


def hidden_rows(key, row_count, salt):
    key_cols = jax.random.fold_in(key, 7)
    key_base = jax.random.fold_in(key, salt)
    key_rows = jax.random.fold_in(key, salt + 100)
    column_scale = jnp.exp(jax.random.uniform(key_cols, (D,), jnp.float32, 0.0, math.log(10.0)))
    row_scale = jnp.exp(jax.random.uniform(key_rows, (row_count, 1), jnp.float32, 0.0, math.log(10.0)))
    base_draw = jnp.clip(jax.random.normal(key_base, (row_count, D), jnp.float32), -4.0, 4.0)
    return (base_draw * column_scale[None, :] * row_scale).astype(jnp.bfloat16)


def draw_question_hidden(key, part):
    return hidden_rows(key, QTOK, 1)


def draw_recomp_hidden(key, part):
    return hidden_rows(key, RECOMP, 2)


def draw_pool_codes(key, part):
    shape_all = (POOL_BLOCKS, 2, BLOCK, KVH * HD)
    values = jax.random.uniform(key, shape_all, jnp.float32, -127.0, 127.0)
    return values.astype(jnp.bfloat16)


def draw_pool_scales(key, part):
    key_base = jax.random.fold_in(key, 1)
    base_scale = jnp.exp(jax.random.uniform(key_base, (POOL_BLOCKS, 2, KVH), jnp.float32, math.log(0.025), math.log(0.05)))
    return base_scale.astype(jnp.bfloat16)


def draw_recomp_pos(key, part):
    key_pick = jax.random.fold_in(key, 11)
    key_order = jax.random.fold_in(key, 12)
    shuffled = jax.random.permutation(key_pick, CTX_TOK - 2)[:RECOMP - 2] + 1
    inner_pos = shuffled.astype(jnp.int32)
    listed = jnp.concatenate([jnp.zeros((1,), jnp.int32), inner_pos, jnp.full((1,), CTX_TOK - 1, jnp.int32)])
    return jax.random.permutation(key_order, listed).astype(jnp.int32)


def plant(array, key, least, top_value):
    longest = array.shape.index(max(array.shape))
    spots = []
    for shift in (0, 1):
        where = [jax.random.randint(jax.random.fold_in(key, axis), (), 0, length) for axis, length in enumerate(array.shape)]
        where[longest] = (where[longest] + shift) % array.shape[longest]
        spots.append(tuple(where))
    return array.at[spots[0]].set(least).at[spots[1]].set(top_value)


def shard_levels(stream_key, extent, shards, least, largest):
    factor_of, own = 1.0, jax.random.fold_in(stream_key, 6)
    for axis_at, parts in shards:
        steps = jnp.exp(jax.random.uniform(jax.random.fold_in(own, axis_at), (parts,), jnp.float32, least / len(shards), largest / len(shards)))
        factor_of = factor_of * jnp.repeat(steps, extent[axis_at] // parts).reshape([-1 if axis == axis_at else 1 for axis in range(len(extent))])
    return factor_of


def routed_block(key, own, number, rows, amount, top, bound, lean):
    sequence = jax.random.permutation(key, amount)
    crowded, usual = portions_of(amount, rows * top, bound, lean, True), portions_of(amount, rows * top, bound, lean, False)
    places = jnp.arange(amount)

    def named(tallies, offset_by):
        used = int((tallies > 0).sum())
        fixed = max(1, used // 4)
        shifted = fixed + (places - fixed + offset_by * (used - fixed)) % max(1, amount - fixed)
        return jnp.zeros((amount,), jnp.int32).at[sequence[jnp.where(places < fixed, places, shifted)]].set(jnp.asarray(tallies, jnp.int32))

    tallies = jnp.where(number % 4 == 0, named(crowded, number // 4), named(usual, number - number // 4 - 1))
    mixed = jax.random.permutation(jax.random.fold_in(own, 3), amount)
    source_of, sink = mixed[0:amount // 2 * 2:2], mixed[1:amount // 2 * 2:2]
    slack = jnp.minimum(tallies[source_of] - 1, bound - tallies[sink]) // 2
    slack = jnp.where((source_of == sequence[0]) | (sink == sequence[0]) | (tallies[sink] == 0), 0, jnp.maximum(slack, 0))
    shifted = jax.random.randint(jax.random.fold_in(own, 4), (amount // 2,), 0, 1 << 20) % (slack + 1)
    tallies = tallies.at[source_of].add(-shifted).at[sink].add(shifted)
    members = jnp.searchsorted(jnp.cumsum(tallies), jnp.arange(rows * top), side="right").astype(jnp.int32)
    grid = members.reshape(top, rows).T
    grid = grid[jax.random.permutation(jax.random.fold_in(own, 1), rows)]
    offset_by = jax.random.randint(jax.random.fold_in(own, 2), (rows, 1), 0, top)
    return jnp.take_along_axis(grid, (jnp.arange(top)[None, :] + offset_by) % top, axis=1)


def portions_of(count, total, bound, lean, full):
    loads = [(1 << 20) // math.isqrt(grade ** lean) + 1 for grade in range(1, count + 1)]
    largest = bound if full else min(bound, max(-(-total // count), total * loads[0] // sum(loads)))
    least = 1 if total - largest >= count - 1 else 0
    counts, spare = [largest] + [least] * (count - 1), total - largest - least * (count - 1)
    while spare > 0:
        free = [i for i in range(1, count) if counts[i] < largest] or [i for i in range(1, count) if counts[i] < bound]
        pool, left = sum([loads[i] for i in free]), spare
        for i in free:
            addition = min(bound - counts[i], max(1, left * loads[i] // pool), spare)
            counts[i] = counts[i] + addition
            spare = spare - addition
    return np.array(counts)


def normal_values(key, shape, width, limit, split=(), held_as=jnp.bfloat16):
    array = width * jax.random.normal(key, shape, jnp.float32)
    if split:
        array = array * shard_levels(key, shape, split, -0.22, 0.18)
    return jnp.clip(array, -limit, limit).astype(held_as)


def setup_inputs(seed: int = 0, part: int = 0) -> dict:
    key_of = jax.random.split(jax.random.key(seed), 11)
    own_keys = jax.random.split(jax.random.fold_in(key_of[10], part), 11)
    question_hidden = draw_question_hidden(jax.random.fold_in(jax.random.fold_in(key_of[10], part), 71), part)
    recomp_hidden = draw_recomp_hidden(jax.random.fold_in(jax.random.fold_in(key_of[10], part), 71), part)
    norm_gain = jnp.clip(1.0 + 0.18 * jax.random.normal(key_of[2], (D,), jnp.float32), 0.099609375, 1.8984375).astype(jnp.bfloat16)
    w_query = normal_values(key_of[3], (D, NH * HD), D ** -0.5, 0.0625, ((0, 4), (1, 4)))
    w_keyval = normal_values(key_of[4], (D, 2, KVH * HD), (D // 16) ** -0.5, 0.25, ((0, 4), (2, 4)))
    pool_codes = draw_pool_codes(jax.random.fold_in(jax.random.fold_in(key_of[10], part), 71), part)
    pool_scales = draw_pool_scales(jax.random.fold_in(jax.random.fold_in(key_of[10], part), 71), part)
    block_owner_keys = jax.random.split(jax.random.fold_in(own_keys[7], 1), CTX_BLOCKS // BLK_DEV)
    block_owner_turns = jax.random.permutation(jax.random.fold_in(own_keys[7], 3), CTX_BLOCKS // BLK_DEV)
    block_owner = jax.vmap(lambda own, number: routed_block(jax.random.fold_in(own_keys[7], 2), own, number, BLK_DEV, OWNERS, 1, MOST, 2))(block_owner_keys, block_owner_turns).reshape((CTX_BLOCKS, 1))
    block_slot = plant(jax.random.randint(own_keys[8], (CTX_BLOCKS,), 0, POOL_DEV), jax.random.fold_in(own_keys[8], 1), 0, POOL_DEV - 1).astype(jnp.int32)
    recomp_pos = draw_recomp_pos(jax.random.fold_in(jax.random.fold_in(key_of[10], part), 71), part)
    return dict(question_hidden=question_hidden, recomp_hidden=recomp_hidden, norm_gain=norm_gain, w_query=w_query, w_keyval=w_keyval, pool_codes=pool_codes, pool_scales=pool_scales, block_owner=block_owner, block_slot=block_slot, recomp_pos=recomp_pos)


norm_eps = 1e-05

def rms_rows(hidden, norm_gain):
    floats = hidden.astype(jnp.float32)
    factor = lax.rsqrt(lax.optimization_barrier(jnp.mean(floats * floats, axis=-1, keepdims=True)) + norm_eps)
    return (floats * factor * norm_gain.astype(jnp.float32)).astype(jnp.bfloat16)

def reference(question_hidden, recomp_hidden, norm_gain, w_query, w_keyval, pool_codes, pool_scales, block_owner, block_slot, recomp_pos):
    kv_width = KVH * HD
    normed_question = rms_rows(question_hidden, norm_gain)
    normed_recomp = rms_rows(recomp_hidden, norm_gain)
    query = jnp.dot(normed_question, w_query, preferred_element_type=jnp.float32).astype(jnp.bfloat16)
    kv_weight = w_keyval.reshape(D, 2 * kv_width)
    question_kv = jnp.dot(normed_question, kv_weight, preferred_element_type=jnp.float32).astype(jnp.bfloat16).reshape(QTOK, 2, kv_width)
    recomp_kv = jnp.dot(normed_recomp, kv_weight, preferred_element_type=jnp.float32).astype(jnp.bfloat16).reshape(RECOMP, 2, kv_width)
    pool_block = (block_owner[:, 0] * POOL_DEV + block_slot).astype(jnp.int32)
    got_codes = jnp.take(pool_codes, pool_block, axis=0).astype(jnp.float32).reshape(CTX_BLOCKS, 2, BLOCK, KVH, HD)
    got_scales = jnp.take(pool_scales, pool_block, axis=0).astype(jnp.float32)
    cached = (got_codes * got_scales[:, :, None, :, None]).astype(jnp.bfloat16)
    cached = jnp.transpose(cached.reshape(CTX_BLOCKS, 2, BLOCK, kv_width), (1, 0, 2, 3)).reshape(2, CTX_TOK, kv_width)
    kv_cache = cached.at[:, recomp_pos.astype(jnp.int32), :].set(jnp.transpose(recomp_kv, (1, 0, 2)))
    key_rows = jnp.concatenate([kv_cache[0], question_kv[:, 0]], axis=0).astype(jnp.float32)
    val_rows = jnp.concatenate([kv_cache[1], question_kv[:, 1]], axis=0).astype(jnp.float32)
    key_index = jnp.arange(CTX_TOK + QTOK, dtype=jnp.int32)
    token_index = jnp.arange(QTOK, dtype=jnp.int32)
    visible = (key_index[None, :] < CTX_TOK) | (key_index[None, :] - CTX_TOK <= token_index[:, None])
    score_scale = HD ** (-0.5)

    def one_head(head_index):
        kv_head = head_index // GROUP
        q_head = lax.dynamic_slice_in_dim(query, head_index * HD, HD, 1).astype(jnp.float32)
        k_head = lax.dynamic_slice_in_dim(key_rows, kv_head * HD, HD, 1)
        v_head = lax.dynamic_slice_in_dim(val_rows, kv_head * HD, HD, 1)
        scores = jnp.dot(q_head, k_head.T, precision=lax.Precision.HIGHEST) * score_scale
        scores = jnp.where(visible, scores, -jnp.inf)
        row_max = lax.optimization_barrier(jnp.max(scores, axis=-1, keepdims=True))
        weights = jnp.where(visible, jnp.exp(scores - row_max), 0.0)
        row_total = lax.optimization_barrier(jnp.sum(weights, axis=-1, keepdims=True))
        weights_low = lax.optimization_barrier(weights.astype(jnp.bfloat16)).astype(jnp.float32)
        summed = jnp.dot(weights_low, v_head, precision=lax.Precision.HIGHEST)
        return (summed / row_total).astype(jnp.bfloat16)
    heads = lax.map(one_head, jnp.arange(NH, dtype=jnp.int32))
    attended = jnp.transpose(heads, (1, 0, 2)).reshape(QTOK, NH * HD)
    return (attended, kv_cache)
```

```python
import functools

import jax
import jax.numpy as jnp
from jax import lax
from jax.experimental import pallas as pl
from jax.sharding import PartitionSpec as P

HD = 128


norm_eps = 1e-05
neg_large = -1e30


def rms_rows(hidden, norm_gain):
    floats = hidden.astype(jnp.float32)
    factor = lax.rsqrt(jnp.mean(floats * floats, axis=-1, keepdims=True) + norm_eps)
    return (floats * factor * norm_gain.astype(jnp.float32)).astype(jnp.bfloat16)


def attn_kernel(rank_ref, q_ref, k_ref, v_ref, o_ref, m_ref, l_ref, *, score_scale):
    tq = q_ref.shape[0]
    first = pl.program_id(0) * tq
    scores = (
        lax.dot_general(
            q_ref[...], k_ref[...], (((1,), (1,)), ((), ())), preferred_element_type=jnp.float32
        )
        * score_scale
    )
    token = first + lax.broadcasted_iota(jnp.int32, scores.shape, 0)
    shown = rank_ref[...] <= token
    masked = jnp.where(shown, scores, neg_large)
    row_max = jnp.max(masked, axis=1, keepdims=True)
    weights = jnp.where(shown, jnp.exp(masked - row_max), 0.0)
    m_ref[...] = row_max
    l_ref[...] = jnp.sum(weights, axis=1, keepdims=True)
    o_ref[...] = jnp.dot(
        weights.astype(jnp.bfloat16), v_ref[...], preferred_element_type=jnp.float32
    )


def attend(queries, keys, vals, key_rank, group_size, score_scale):
    tokens, q_width = queries.shape
    key_count = keys.shape[0]
    heads = q_width // HD
    tq = min(tokens, 128)
    grid = (tokens // tq, heads)
    return pl.pallas_call(
        functools.partial(attn_kernel, score_scale=score_scale),
        grid=grid,
        in_specs=[
            pl.BlockSpec((1, key_count), lambda i, n: (0, 0)),
            pl.BlockSpec((tq, HD), lambda i, n: (i, n)),
            pl.BlockSpec((key_count, HD), lambda i, n: (0, n // group_size)),
            pl.BlockSpec((key_count, HD), lambda i, n: (0, n // group_size)),
        ],
        out_specs=[
            pl.BlockSpec((tq, HD), lambda i, n: (i, n)),
            pl.BlockSpec((None, tq, 1), lambda i, n: (n, i, 0)),
            pl.BlockSpec((None, tq, 1), lambda i, n: (n, i, 0)),
        ],
        out_shape=[
            jax.ShapeDtypeStruct((tokens, q_width), jnp.float32),
            jax.ShapeDtypeStruct((heads, tokens, 1), jnp.float32),
            jax.ShapeDtypeStruct((heads, tokens, 1), jnp.float32),
        ],
    )(key_rank, queries, keys, vals)


def body(
    question_hidden,
    recomp_hidden,
    norm_gain,
    w_query,
    w_keyval,
    pool_codes,
    pool_scales,
    block_owner,
    block_slot,
    recomp_pos,
):
    shards = lax.axis_size("ctx")
    own_index = lax.axis_index("ctx")
    q_rows = question_hidden.shape[0]
    r_rows = recomp_hidden.shape[0]
    row_count = q_rows + r_rows
    kv_width = w_keyval.shape[2]
    kv_heads = kv_width // HD
    q_width = w_query.shape[1]
    group_size = q_width // kv_width
    score_scale = HD ** (-0.5)

    owners = block_owner[:, 0].reshape(shards, -1)
    per_dev = owners.shape[1]
    slot_table = block_slot.reshape(shards, per_dev)
    capacity = max(2, 2 * per_dev // shards)
    positions = jnp.arange(per_dev)
    earlier_mask = positions[None, :] < positions[:, None]
    same_owner = owners[:, :, None] == owners[:, None, :]
    order_rank = jnp.sum((same_owner & earlier_mask[None]).astype(jnp.int32), axis=2)
    slot_ids = jnp.arange(capacity)
    chosen = (owners == own_index)[:, :, None] & (order_rank[:, :, None] == slot_ids[None, None, :])
    send_slot = jnp.sum(jnp.where(chosen, slot_table[:, :, None], 0), axis=1).reshape(-1)
    send_codes = jnp.take(pool_codes, send_slot, axis=0).reshape(
        (shards, capacity) + pool_codes.shape[1:]
    )
    send_scales = jnp.take(pool_scales, send_slot, axis=0).reshape(
        (shards, capacity) + pool_scales.shape[1:]
    )
    got_codes, got_scales = (
        lax.all_to_all(send_codes, "ctx", split_axis=0, concat_axis=0, tiled=True),
        lax.all_to_all(send_scales, "ctx", split_axis=0, concat_axis=0, tiled=True),
    )

    normed = jnp.concatenate(
        [rms_rows(question_hidden, norm_gain), rms_rows(recomp_hidden, norm_gain)], axis=0
    )
    pieces = lax.all_to_all(normed, "ctx", split_axis=1, concat_axis=0, tiled=True)
    width_part = pieces.shape[1]
    arranged = pieces.reshape(shards, row_count, width_part)
    question_part = arranged[:, :q_rows, :].reshape(shards * q_rows, width_part)
    kv_weight = w_keyval.reshape(w_keyval.shape[0], 2 * kv_width)
    query_part = jnp.dot(question_part, w_query, preferred_element_type=jnp.float32)
    kv_part = jnp.dot(pieces, kv_weight, preferred_element_type=jnp.float32)
    query_sum, kv_sum = lax.psum((query_part, kv_part), "ctx")
    every_query = query_sum.astype(jnp.bfloat16)
    every_kv = kv_sum.astype(jnp.bfloat16).reshape(shards, row_count, 2, kv_width)
    question_kv = lax.dynamic_index_in_dim(every_kv, own_index, 0, keepdims=False)[:q_rows]
    recomp_kv = every_kv[:, q_rows:].reshape(shards * r_rows, 2, kv_width)

    own_owner = lax.dynamic_index_in_dim(owners, own_index, 0, keepdims=False)
    own_rank = lax.dynamic_index_in_dim(order_rank, own_index, 0, keepdims=False)
    flat_index = own_owner * capacity + own_rank
    block_codes = jnp.take(
        got_codes.reshape((shards * capacity,) + pool_codes.shape[1:]), flat_index, axis=0
    )
    block_scales = jnp.take(
        got_scales.reshape((shards * capacity,) + pool_scales.shape[1:]), flat_index, axis=0
    )
    block_len = block_codes.shape[2]
    dequant = (
        block_codes.astype(jnp.float32).reshape(per_dev, 2, block_len, kv_heads, HD)
        * block_scales.astype(jnp.float32)[:, :, None, :, None]
    )
    ctx_dev = per_dev * block_len
    cached = jnp.transpose(
        dequant.astype(jnp.bfloat16).reshape(per_dev, 2, block_len, kv_width), (1, 0, 2, 3)
    ).reshape(2, ctx_dev, kv_width)

    local_pos = recomp_pos - own_index * ctx_dev
    match = local_pos[None, :] == jnp.arange(ctx_dev)[:, None]
    hit = jnp.any(match, axis=1)
    one_hot = match.astype(jnp.bfloat16)
    placed = jnp.einsum(
        "pi,ick->cpk", one_hot, recomp_kv, preferred_element_type=jnp.float32
    ).astype(jnp.bfloat16)
    kv_cache = jnp.where(hit[None, :, None], placed, cached)

    key_local = jnp.concatenate([kv_cache[0], question_kv[:, 0]], axis=0)
    val_local = jnp.concatenate([kv_cache[1], question_kv[:, 1]], axis=0)
    key_span = ctx_dev + q_rows
    key_offset = jnp.arange(key_span)
    key_rank = jnp.where(
        key_offset < ctx_dev, -1, own_index * q_rows + key_offset - ctx_dev
    ).astype(jnp.int32)[None, :]

    part_sums, part_max, part_total = attend(
        every_query, key_local, val_local, key_rank, group_size, score_scale
    )
    heads = q_width // HD

    def by_token(value):
        return jnp.transpose(value[:, :, 0]).reshape(shards, q_rows, heads)

    sent = (
        part_sums.reshape(shards, q_rows, q_width),
        by_token(part_max),
        by_token(part_total),
    )
    got_sums, got_max, got_total = (
        lax.all_to_all(sent[0], "ctx", split_axis=0, concat_axis=0, tiled=True),
        lax.all_to_all(sent[1], "ctx", split_axis=0, concat_axis=0, tiled=True),
        lax.all_to_all(sent[2], "ctx", split_axis=0, concat_axis=0, tiled=True),
    )
    best_max = jnp.max(got_max, axis=0)
    factor = jnp.exp(got_max - best_max[None])
    row_total = jnp.sum(got_total * factor, axis=0)
    weighted = jnp.sum(
        got_sums.reshape(shards, q_rows, heads, HD) * factor[..., None], axis=0
    )
    attended = (weighted / row_total[..., None]).reshape(q_rows, q_width).astype(jnp.bfloat16)
    return (attended, kv_cache)


def solution(mesh):
    placed = (
        P(("groups", "ctx"), None),
        P(("groups", "ctx"), None),
        P(),
        P("ctx", "tp"),
        P("ctx", None, "tp"),
        P(("groups", "ctx"), None, None, "tp"),
        P(("groups", "ctx"), None, "tp"),
        P("groups", None),
        P("groups"),
        P("groups"),
    )
    return jax.shard_map(
        body,
        mesh=mesh,
        in_specs=placed,
        out_specs=(P(("groups", "ctx"), "tp"), P(None, ("groups", "ctx"), "tp")),
        check_vma=False,
    )
```

```python
import functools

import jax
import jax.numpy as jnp
from jax import lax
from jax.experimental import pallas as pl
from jax.sharding import PartitionSpec as P

HD = 128


norm_eps = 1e-05
neg_large = -1e30


def rms_rows(hidden, norm_gain):
    floats = hidden.astype(jnp.float32)
    factor = lax.rsqrt(jnp.mean(floats * floats, axis=-1, keepdims=True) + norm_eps)
    return (floats * factor * norm_gain.astype(jnp.float32)).astype(jnp.bfloat16)


def attn_kernel(rank_ref, q_ref, k_ref, v_ref, o_ref, m_ref, l_ref, *, score_scale, ctx_keys):
    tq = q_ref.shape[0]
    first = pl.program_id(0) * tq
    dims = (((1,), (1,)), ((), ()))
    queries = q_ref[...]
    ctx_scores = (
        lax.dot_general(queries, k_ref[:ctx_keys, :], dims, preferred_element_type=jnp.float32)
        * score_scale
    )
    own_scores = (
        lax.dot_general(queries, k_ref[ctx_keys:, :], dims, preferred_element_type=jnp.float32)
        * score_scale
    )
    token = first + lax.broadcasted_iota(jnp.int32, own_scores.shape, 0)
    shown = rank_ref[...] <= token
    own_masked = jnp.where(shown, own_scores, neg_large)
    row_max = jnp.maximum(
        jnp.max(ctx_scores, axis=1, keepdims=True), jnp.max(own_masked, axis=1, keepdims=True)
    )
    ctx_weights = jnp.exp(ctx_scores - row_max)
    own_weights = jnp.where(shown, jnp.exp(own_masked - row_max), 0.0)
    m_ref[...] = row_max
    l_ref[...] = jnp.sum(ctx_weights, axis=1, keepdims=True) + jnp.sum(
        own_weights, axis=1, keepdims=True
    )
    o_ref[...] = jnp.dot(
        ctx_weights.astype(jnp.bfloat16), v_ref[:ctx_keys, :], preferred_element_type=jnp.float32
    ) + jnp.dot(
        own_weights.astype(jnp.bfloat16), v_ref[ctx_keys:, :], preferred_element_type=jnp.float32
    )


def attend(queries, keys, vals, key_rank, ctx_keys, group_size, score_scale):
    tokens, q_width = queries.shape
    key_count = keys.shape[0]
    heads = q_width // HD
    tq = min(tokens, 128)
    grid = (tokens // tq, heads)
    return pl.pallas_call(
        functools.partial(attn_kernel, score_scale=score_scale, ctx_keys=ctx_keys),
        grid=grid,
        in_specs=[
            pl.BlockSpec((1, key_count - ctx_keys), lambda i, n: (0, 0)),
            pl.BlockSpec((tq, HD), lambda i, n: (i, n)),
            pl.BlockSpec((key_count, HD), lambda i, n: (0, n // group_size)),
            pl.BlockSpec((key_count, HD), lambda i, n: (0, n // group_size)),
        ],
        out_specs=[
            pl.BlockSpec((tq, HD), lambda i, n: (i, n)),
            pl.BlockSpec((None, tq, 1), lambda i, n: (n, i, 0)),
            pl.BlockSpec((None, tq, 1), lambda i, n: (n, i, 0)),
        ],
        out_shape=[
            jax.ShapeDtypeStruct((tokens, q_width), jnp.float32),
            jax.ShapeDtypeStruct((heads, tokens, 1), jnp.float32),
            jax.ShapeDtypeStruct((heads, tokens, 1), jnp.float32),
        ],
    )(key_rank, queries, keys, vals)


def body(
    question_hidden,
    recomp_hidden,
    norm_gain,
    w_query,
    w_keyval,
    pool_codes,
    pool_scales,
    block_owner,
    block_slot,
    recomp_pos,
):
    shards = lax.axis_size("ctx")
    own_index = lax.axis_index("ctx")
    q_rows = question_hidden.shape[0]
    r_rows = recomp_hidden.shape[0]
    row_count = q_rows + r_rows
    kv_width = w_keyval.shape[2]
    kv_heads = kv_width // HD
    q_width = w_query.shape[1]
    heads = q_width // HD
    group_size = q_width // kv_width
    score_scale = HD ** (-0.5)

    owners = block_owner[:, 0].reshape(shards, -1)
    per_dev = owners.shape[1]
    slot_table = block_slot.reshape(shards, per_dev)
    capacity = max(2, 2 * per_dev // shards)
    positions = jnp.arange(per_dev)
    earlier_mask = positions[None, :] < positions[:, None]
    same_owner = owners[:, :, None] == owners[:, None, :]
    order_rank = jnp.sum((same_owner & earlier_mask[None]).astype(jnp.int32), axis=2)
    slot_ids = jnp.arange(capacity)
    chosen = (owners == own_index)[:, :, None] & (order_rank[:, :, None] == slot_ids[None, None, :])
    send_slot = jnp.sum(jnp.where(chosen, slot_table[:, :, None], 0), axis=1).reshape(-1)
    block_len = pool_codes.shape[2]
    send_codes = jnp.take(pool_codes, send_slot, axis=0)
    send_scales = jnp.take(pool_scales, send_slot, axis=0)
    send_blocks = (
        send_codes.astype(jnp.float32).reshape(shards * capacity, 2, block_len, kv_heads, HD)
        * send_scales.astype(jnp.float32)[:, :, None, :, None]
    ).astype(jnp.bfloat16).reshape((shards, capacity, 2, block_len, kv_width))
    got_blocks = lax.all_to_all(send_blocks, "ctx", split_axis=0, concat_axis=0, tiled=True)

    normed = jnp.concatenate(
        [rms_rows(question_hidden, norm_gain), rms_rows(recomp_hidden, norm_gain)], axis=0
    )
    pieces = lax.all_to_all(normed, "ctx", split_axis=1, concat_axis=0, tiled=True)
    width_part = pieces.shape[1]
    arranged = pieces.reshape(shards, row_count, width_part)
    question_part = arranged[:, :q_rows, :].reshape(shards * q_rows, width_part)
    kv_weight = w_keyval.reshape(w_keyval.shape[0], 2 * kv_width)
    query_part = jnp.dot(question_part, w_query, preferred_element_type=jnp.float32)
    kv_part = jnp.dot(pieces, kv_weight, preferred_element_type=jnp.float32)

    q_size = q_rows * q_width
    partials = jnp.concatenate(
        [query_part.reshape(shards, q_size), kv_part.reshape(shards, row_count * 2 * kv_width)],
        axis=1,
    )
    summed = jnp.sum(
        lax.all_to_all(partials, "ctx", split_axis=0, concat_axis=0, tiled=True), axis=0
    ).astype(jnp.bfloat16)
    gathered = lax.all_gather(summed, "ctx", axis=0, tiled=False)
    every_query = gathered[:, :q_size].reshape(shards * q_rows, q_width)
    every_kv = gathered[:, q_size:].reshape(shards, row_count, 2, kv_width)
    question_kv = summed[q_size:].reshape(row_count, 2, kv_width)[:q_rows]
    recomp_kv = every_kv[:, q_rows:].reshape(shards * r_rows, 2, kv_width)

    own_owner = lax.dynamic_index_in_dim(owners, own_index, 0, keepdims=False)
    own_rank = lax.dynamic_index_in_dim(order_rank, own_index, 0, keepdims=False)
    flat_index = own_owner * capacity + own_rank
    block_rows = jnp.take(
        got_blocks.reshape((shards * capacity, 2, block_len, kv_width)), flat_index, axis=0
    )
    ctx_dev = per_dev * block_len
    cached = jnp.transpose(block_rows, (1, 0, 2, 3)).reshape(2, ctx_dev, kv_width)

    local_pos = recomp_pos - own_index * ctx_dev
    match = local_pos[None, :] == jnp.arange(ctx_dev)[:, None]
    hit = jnp.any(match, axis=1)
    one_hot = match.astype(jnp.bfloat16)
    placed = jnp.einsum(
        "pi,ick->cpk", one_hot, recomp_kv, preferred_element_type=jnp.float32
    ).astype(jnp.bfloat16)
    kv_cache = jnp.where(hit[None, :, None], placed, cached)

    key_local = jnp.concatenate([kv_cache[0], question_kv[:, 0]], axis=0)
    val_local = jnp.concatenate([kv_cache[1], question_kv[:, 1]], axis=0)
    key_rank = (own_index * q_rows + jnp.arange(q_rows)).astype(jnp.int32)[None, :]

    part_sums, part_max, part_total = attend(
        every_query, key_local, val_local, key_rank, ctx_dev, group_size, score_scale
    )

    def by_token(value):
        return jnp.transpose(value[:, :, 0]).reshape(shards, q_rows, heads)

    sent = jnp.concatenate(
        [part_sums.reshape(shards, q_rows, q_width), by_token(part_max), by_token(part_total)],
        axis=2,
    )
    got = lax.all_to_all(sent, "ctx", split_axis=0, concat_axis=0, tiled=True)
    got_sums = got[:, :, :q_width]
    got_max = got[:, :, q_width : q_width + heads]
    got_total = got[:, :, q_width + heads :]
    best_max = jnp.max(got_max, axis=0)
    factor = jnp.exp(got_max - best_max[None])
    row_total = jnp.sum(got_total * factor, axis=0)
    weighted = jnp.sum(
        got_sums.reshape(shards, q_rows, heads, HD) * factor[..., None], axis=0
    )
    attended = (weighted / row_total[..., None]).reshape(q_rows, q_width).astype(jnp.bfloat16)
    return (attended, kv_cache)


def solution(mesh):
    placed = (
        P(("groups", "ctx"), None),
        P(("groups", "ctx"), None),
        P(),
        P("ctx", "tp"),
        P("ctx", None, "tp"),
        P(("groups", "ctx"), None, None, "tp"),
        P(("groups", "ctx"), None, "tp"),
        P("groups", None),
        P("groups"),
        P("groups"),
    )
    return jax.shard_map(
        body,
        mesh=mesh,
        in_specs=placed,
        out_specs=(P(("groups", "ctx"), "tp"), P(None, ("groups", "ctx"), "tp")),
        check_vma=False,
    )
```

```python
import functools

import jax
import jax.numpy as jnp
from jax import lax
from jax.experimental import pallas as pl
from jax.sharding import PartitionSpec as P

HD = 128


norm_eps = 1e-05
neg_large = -1e30


def rms_rows(hidden, norm_gain):
    floats = hidden.astype(jnp.float32)
    factor = lax.rsqrt(jnp.mean(floats * floats, axis=-1, keepdims=True) + norm_eps)
    return (floats * factor * norm_gain.astype(jnp.float32)).astype(jnp.bfloat16)


def attn_kernel(rank_ref, q_ref, k_ref, v_ref, o_ref, m_ref, l_ref, *, score_scale, ctx_keys):
    tq = q_ref.shape[0]
    first = pl.program_id(0) * tq
    dims = (((1,), (1,)), ((), ()))
    queries = q_ref[...]
    ctx_scores = (
        lax.dot_general(queries, k_ref[:ctx_keys, :], dims, preferred_element_type=jnp.float32)
        * score_scale
    )
    own_scores = (
        lax.dot_general(queries, k_ref[ctx_keys:, :], dims, preferred_element_type=jnp.float32)
        * score_scale
    )
    token = first + lax.broadcasted_iota(jnp.int32, own_scores.shape, 0)
    shown = rank_ref[...] <= token
    own_masked = jnp.where(shown, own_scores, neg_large)
    row_max = jnp.maximum(
        jnp.max(ctx_scores, axis=1, keepdims=True), jnp.max(own_masked, axis=1, keepdims=True)
    )
    ctx_weights = jnp.exp(ctx_scores - row_max)
    own_weights = jnp.where(shown, jnp.exp(own_masked - row_max), 0.0)
    m_ref[...] = row_max
    l_ref[...] = jnp.sum(ctx_weights, axis=1, keepdims=True) + jnp.sum(
        own_weights, axis=1, keepdims=True
    )
    o_ref[...] = jnp.dot(
        ctx_weights.astype(jnp.bfloat16), v_ref[:ctx_keys, :], preferred_element_type=jnp.float32
    ) + jnp.dot(
        own_weights.astype(jnp.bfloat16), v_ref[ctx_keys:, :], preferred_element_type=jnp.float32
    )


def attend(queries, keys, vals, key_rank, ctx_keys, group_size, score_scale):
    tokens, q_width = queries.shape
    key_count = keys.shape[0]
    heads = q_width // HD
    tq = min(tokens, 128)
    grid = (tokens // tq, heads)
    return pl.pallas_call(
        functools.partial(attn_kernel, score_scale=score_scale, ctx_keys=ctx_keys),
        grid=grid,
        in_specs=[
            pl.BlockSpec((1, key_count - ctx_keys), lambda i, n: (0, 0)),
            pl.BlockSpec((tq, HD), lambda i, n: (i, n)),
            pl.BlockSpec((key_count, HD), lambda i, n: (0, n // group_size)),
            pl.BlockSpec((key_count, HD), lambda i, n: (0, n // group_size)),
        ],
        out_specs=[
            pl.BlockSpec((tq, HD), lambda i, n: (i, n)),
            pl.BlockSpec((None, tq, 1), lambda i, n: (n, i, 0)),
            pl.BlockSpec((None, tq, 1), lambda i, n: (n, i, 0)),
        ],
        out_shape=[
            jax.ShapeDtypeStruct((tokens, q_width), jnp.float32),
            jax.ShapeDtypeStruct((heads, tokens, 1), jnp.float32),
            jax.ShapeDtypeStruct((heads, tokens, 1), jnp.float32),
        ],
    )(key_rank, queries, keys, vals)


def shift_pairs(shards, step):
    chips = shards // 2
    return [(i, ((i // 2 + step) % chips) * 2 + i % 2) for i in range(shards)]


def core_pairs(shards):
    return [(i, i ^ 1) for i in range(shards)]


def pick_core(pair, core):
    return jnp.take(pair, jnp.arange(2) ^ core, axis=1)


def hier_reduce_gather(partials, shards, own_index):
    chips = shards // 2
    core = own_index % 2
    chip = own_index // 2
    by_core = partials.reshape(chips, 2, -1)
    mine = lax.dynamic_index_in_dim(by_core, core, 1, keepdims=False)
    other = lax.dynamic_index_in_dim(by_core, 1 - core, 1, keepdims=False)
    chip_sum = mine + lax.ppermute(other, "ctx", core_pairs(shards))
    total = lax.dynamic_index_in_dim(chip_sum, chip, 0, keepdims=False)
    for step in range(1, chips):
        send = lax.dynamic_index_in_dim(chip_sum, (chip + step) % chips, 0, keepdims=False)
        total = total + lax.ppermute(send, "ctx", shift_pairs(shards, step))
    rounded = total.astype(jnp.bfloat16)
    got = [rounded] + [
        lax.ppermute(rounded, "ctx", shift_pairs(shards, step)) for step in range(1, chips)
    ]
    by_shift = jnp.stack(got)
    by_chip = jnp.take(by_shift, (chip - jnp.arange(chips)) % chips, axis=0)
    pair = jnp.stack([by_chip, lax.ppermute(by_chip, "ctx", core_pairs(shards))], axis=1)
    return pick_core(pair, core).reshape(shards, -1)


def merge(parts, sums_width):
    sums = [p[..., :sums_width] for p in parts]
    maxes = [p[..., sums_width:sums_width + (p.shape[-1] - sums_width) // 2] for p in parts]
    totals = [p[..., sums_width + (p.shape[-1] - sums_width) // 2:] for p in parts]
    best = maxes[0]
    for m in maxes[1:]:
        best = jnp.maximum(best, m)
    factors = [jnp.exp(m - best) for m in maxes]
    heads = best.shape[-1]
    lead = sums[0].shape[:-1]
    out_sum = sum(
        s.reshape(lead + (heads, HD)) * f[..., None] for s, f in zip(sums, factors)
    ).reshape(lead + (sums_width,))
    out_total = sum(t * f for t, f in zip(totals, factors))
    return jnp.concatenate([out_sum, best, out_total], axis=-1)


def hier_combine(sent, shards, own_index, sums_width):
    chips = shards // 2
    core = own_index % 2
    chip = own_index // 2
    by_core = sent.reshape((chips, 2) + sent.shape[1:])
    mine = lax.dynamic_index_in_dim(by_core, core, 1, keepdims=False)
    other = lax.dynamic_index_in_dim(by_core, 1 - core, 1, keepdims=False)
    chip_merged = merge([mine, lax.ppermute(other, "ctx", core_pairs(shards))], sums_width)
    parts = [lax.dynamic_index_in_dim(chip_merged, chip, 0, keepdims=False)]
    for step in range(1, chips):
        send = lax.dynamic_index_in_dim(chip_merged, (chip + step) % chips, 0, keepdims=False)
        parts.append(lax.ppermute(send, "ctx", shift_pairs(shards, step)))
    return merge(parts, sums_width)


def body(
    question_hidden,
    recomp_hidden,
    norm_gain,
    w_query,
    w_keyval,
    pool_codes,
    pool_scales,
    block_owner,
    block_slot,
    recomp_pos,
):
    shards = lax.axis_size("ctx")
    own_index = lax.axis_index("ctx")
    q_rows = question_hidden.shape[0]
    r_rows = recomp_hidden.shape[0]
    row_count = q_rows + r_rows
    kv_width = w_keyval.shape[2]
    kv_heads = kv_width // HD
    q_width = w_query.shape[1]
    heads = q_width // HD
    group_size = q_width // kv_width
    score_scale = HD ** (-0.5)

    owners = block_owner[:, 0].reshape(shards, -1)
    per_dev = owners.shape[1]
    slot_table = block_slot.reshape(shards, per_dev)
    capacity = max(2, 2 * per_dev // shards)
    positions = jnp.arange(per_dev)
    earlier_mask = positions[None, :] < positions[:, None]
    same_owner = owners[:, :, None] == owners[:, None, :]
    order_rank = jnp.sum((same_owner & earlier_mask[None]).astype(jnp.int32), axis=2)
    slot_ids = jnp.arange(capacity)
    chosen = (owners == own_index)[:, :, None] & (order_rank[:, :, None] == slot_ids[None, None, :])
    send_slot = jnp.sum(jnp.where(chosen, slot_table[:, :, None], 0), axis=1).reshape(-1)
    block_len = pool_codes.shape[2]
    send_codes = jnp.take(pool_codes, send_slot, axis=0)
    send_scales = jnp.take(pool_scales, send_slot, axis=0)
    send_blocks = (
        send_codes.astype(jnp.float32).reshape(shards * capacity, 2, block_len, kv_heads, HD)
        * send_scales.astype(jnp.float32)[:, :, None, :, None]
    ).astype(jnp.bfloat16).reshape((shards, capacity, 2, block_len, kv_width))
    got_blocks = lax.all_to_all(send_blocks, "ctx", split_axis=0, concat_axis=0, tiled=True)

    normed = jnp.concatenate(
        [rms_rows(question_hidden, norm_gain), rms_rows(recomp_hidden, norm_gain)], axis=0
    )
    pieces = lax.all_to_all(normed, "ctx", split_axis=1, concat_axis=0, tiled=True)
    width_part = pieces.shape[1]
    arranged = pieces.reshape(shards, row_count, width_part)
    question_part = arranged[:, :q_rows, :].reshape(shards * q_rows, width_part)
    kv_weight = w_keyval.reshape(w_keyval.shape[0], 2 * kv_width)
    query_part = jnp.dot(question_part, w_query, preferred_element_type=jnp.float32)
    kv_part = jnp.dot(pieces, kv_weight, preferred_element_type=jnp.float32)

    q_size = q_rows * q_width
    partials = jnp.concatenate(
        [query_part.reshape(shards, q_size), kv_part.reshape(shards, row_count * 2 * kv_width)],
        axis=1,
    )
    gathered = hier_reduce_gather(partials, shards, own_index)
    summed = lax.dynamic_index_in_dim(gathered, own_index, 0, keepdims=False)
    every_query = gathered[:, :q_size].reshape(shards * q_rows, q_width)
    every_kv = gathered[:, q_size:].reshape(shards, row_count, 2, kv_width)
    question_kv = summed[q_size:].reshape(row_count, 2, kv_width)[:q_rows]
    recomp_kv = every_kv[:, q_rows:].reshape(shards * r_rows, 2, kv_width)

    own_owner = lax.dynamic_index_in_dim(owners, own_index, 0, keepdims=False)
    own_rank = lax.dynamic_index_in_dim(order_rank, own_index, 0, keepdims=False)
    flat_index = own_owner * capacity + own_rank
    block_rows = jnp.take(
        got_blocks.reshape((shards * capacity, 2, block_len, kv_width)), flat_index, axis=0
    )
    ctx_dev = per_dev * block_len
    cached = jnp.transpose(block_rows, (1, 0, 2, 3)).reshape(2, ctx_dev, kv_width)

    local_pos = recomp_pos - own_index * ctx_dev
    match = local_pos[None, :] == jnp.arange(ctx_dev)[:, None]
    hit = jnp.any(match, axis=1)
    one_hot = match.astype(jnp.bfloat16)
    placed = jnp.einsum(
        "pi,ick->cpk", one_hot, recomp_kv, preferred_element_type=jnp.float32
    ).astype(jnp.bfloat16)
    kv_cache = jnp.where(hit[None, :, None], placed, cached)

    key_local = jnp.concatenate([kv_cache[0], question_kv[:, 0]], axis=0)
    val_local = jnp.concatenate([kv_cache[1], question_kv[:, 1]], axis=0)
    key_rank = (own_index * q_rows + jnp.arange(q_rows)).astype(jnp.int32)[None, :]

    part_sums, part_max, part_total = attend(
        every_query, key_local, val_local, key_rank, ctx_dev, group_size, score_scale
    )

    def by_token(value):
        return jnp.transpose(value[:, :, 0]).reshape(shards, q_rows, heads)

    sent = jnp.concatenate(
        [part_sums.reshape(shards, q_rows, q_width), by_token(part_max), by_token(part_total)],
        axis=2,
    )
    got = hier_combine(sent, shards, own_index, q_width)
    weighted = got[:, :q_width].reshape(q_rows, heads, HD)
    row_total = got[:, q_width + heads :]
    attended = (weighted / row_total[..., None]).reshape(q_rows, q_width).astype(jnp.bfloat16)
    return (attended, kv_cache)


def solution(mesh):
    placed = (
        P(("groups", "ctx"), None),
        P(("groups", "ctx"), None),
        P(),
        P("ctx", "tp"),
        P("ctx", None, "tp"),
        P(("groups", "ctx"), None, None, "tp"),
        P(("groups", "ctx"), None, "tp"),
        P("groups", None),
        P("groups"),
        P("groups"),
    )
    return jax.shard_map(
        body,
        mesh=mesh,
        in_specs=placed,
        out_specs=(P(("groups", "ctx"), "tp"), P(None, ("groups", "ctx"), "tp")),
        check_vma=False,
    )
```

```python
import functools

import jax
import jax.numpy as jnp
from jax import lax
from jax.experimental import pallas as pl
from jax.sharding import PartitionSpec as P

HD = 128


norm_eps = 1e-05
neg_large = -1e30


def rms_rows(hidden, norm_gain):
    floats = hidden.astype(jnp.float32)
    factor = lax.rsqrt(jnp.mean(floats * floats, axis=-1, keepdims=True) + norm_eps)
    return (floats * factor * norm_gain.astype(jnp.float32)).astype(jnp.bfloat16)


def attn_kernel(
    bias_ref, rank_ref, q_ref, kc_ref, kq_ref, vc_ref, vq_ref, o_ref, m_ref, l_ref, *, score_scale
):
    tq = q_ref.shape[0]
    first = pl.program_id(0) * tq
    dims = (((1,), (1,)), ((), ()))
    queries = q_ref[...]
    ctx_scores = (
        lax.dot_general(queries, kc_ref[...], dims, preferred_element_type=jnp.float32)
        * score_scale
        + bias_ref[...]
    )
    own_scores = (
        lax.dot_general(queries, kq_ref[...], dims, preferred_element_type=jnp.float32)
        * score_scale
    )
    token = first + lax.broadcasted_iota(jnp.int32, own_scores.shape, 0)
    shown = rank_ref[...] <= token
    own_masked = jnp.where(shown, own_scores, neg_large)
    row_max = jnp.maximum(
        jnp.max(ctx_scores, axis=1, keepdims=True), jnp.max(own_masked, axis=1, keepdims=True)
    )
    ctx_weights = jnp.exp(ctx_scores - row_max)
    own_weights = jnp.where(shown, jnp.exp(own_masked - row_max), 0.0)
    m_ref[...] = row_max
    l_ref[...] = jnp.sum(ctx_weights, axis=1, keepdims=True) + jnp.sum(
        own_weights, axis=1, keepdims=True
    )
    o_ref[...] = jnp.dot(
        ctx_weights.astype(jnp.bfloat16), vc_ref[...], preferred_element_type=jnp.float32
    ) + jnp.dot(own_weights.astype(jnp.bfloat16), vq_ref[...], preferred_element_type=jnp.float32)


def attend(queries, ctx_keys, own_keys, ctx_vals, own_vals, ctx_bias, key_rank, group_size, score_scale):
    tokens, q_width = queries.shape
    ctx_count = ctx_keys.shape[0]
    own_count = own_keys.shape[0]
    heads = q_width // HD
    tq = min(tokens, 128)
    grid = (tokens // tq, heads)
    return pl.pallas_call(
        functools.partial(attn_kernel, score_scale=score_scale),
        grid=grid,
        in_specs=[
            pl.BlockSpec((1, ctx_count), lambda i, n: (0, 0)),
            pl.BlockSpec((1, own_count), lambda i, n: (0, 0)),
            pl.BlockSpec((tq, HD), lambda i, n: (i, n)),
            pl.BlockSpec((ctx_count, HD), lambda i, n: (0, n // group_size)),
            pl.BlockSpec((own_count, HD), lambda i, n: (0, n // group_size)),
            pl.BlockSpec((ctx_count, HD), lambda i, n: (0, n // group_size)),
            pl.BlockSpec((own_count, HD), lambda i, n: (0, n // group_size)),
        ],
        out_specs=[
            pl.BlockSpec((tq, HD), lambda i, n: (i, n)),
            pl.BlockSpec((None, tq, 1), lambda i, n: (n, i, 0)),
            pl.BlockSpec((None, tq, 1), lambda i, n: (n, i, 0)),
        ],
        out_shape=[
            jax.ShapeDtypeStruct((tokens, q_width), jnp.float32),
            jax.ShapeDtypeStruct((heads, tokens, 1), jnp.float32),
            jax.ShapeDtypeStruct((heads, tokens, 1), jnp.float32),
        ],
    )(ctx_bias, key_rank, queries, ctx_keys, own_keys, ctx_vals, own_vals)


def shift_pairs(shards, step):
    chips = shards // 2
    return [(i, ((i // 2 + step) % chips) * 2 + i % 2) for i in range(shards)]


def core_pairs(shards):
    return [(i, i ^ 1) for i in range(shards)]


def pick_core(pair, core):
    return jnp.take(pair, jnp.arange(2) ^ core, axis=1)


def hier_reduce_gather(partials, shards, own_index):
    chips = shards // 2
    core = own_index % 2
    chip = own_index // 2
    by_core = partials.reshape(chips, 2, -1)
    mine = lax.dynamic_index_in_dim(by_core, core, 1, keepdims=False)
    other = lax.dynamic_index_in_dim(by_core, 1 - core, 1, keepdims=False)
    chip_sum = mine + lax.ppermute(other, "ctx", core_pairs(shards))
    total = lax.dynamic_index_in_dim(chip_sum, chip, 0, keepdims=False)
    for step in range(1, chips):
        send = lax.dynamic_index_in_dim(chip_sum, (chip + step) % chips, 0, keepdims=False)
        total = total + lax.ppermute(send, "ctx", shift_pairs(shards, step))
    rounded = total.astype(jnp.bfloat16)
    got = [rounded] + [
        lax.ppermute(rounded, "ctx", shift_pairs(shards, step)) for step in range(1, chips)
    ]
    by_shift = jnp.stack(got)
    by_chip = jnp.take(by_shift, (chip - jnp.arange(chips)) % chips, axis=0)
    pair = jnp.stack([by_chip, lax.ppermute(by_chip, "ctx", core_pairs(shards))], axis=1)
    return pick_core(pair, core).reshape(shards, -1)


def merge(parts, sums_width):
    sums = [p[..., :sums_width] for p in parts]
    maxes = [p[..., sums_width:sums_width + (p.shape[-1] - sums_width) // 2] for p in parts]
    totals = [p[..., sums_width + (p.shape[-1] - sums_width) // 2:] for p in parts]
    best = maxes[0]
    for m in maxes[1:]:
        best = jnp.maximum(best, m)
    factors = [jnp.exp(m - best) for m in maxes]
    heads = best.shape[-1]
    lead = sums[0].shape[:-1]
    out_sum = sum(
        s.reshape(lead + (heads, HD)) * f[..., None] for s, f in zip(sums, factors)
    ).reshape(lead + (sums_width,))
    out_total = sum(t * f for t, f in zip(totals, factors))
    return jnp.concatenate([out_sum, best, out_total], axis=-1)


def hier_combine(sent, shards, own_index, sums_width):
    chips = shards // 2
    core = own_index % 2
    chip = own_index // 2
    by_core = sent.reshape((chips, 2) + sent.shape[1:])
    mine = lax.dynamic_index_in_dim(by_core, core, 1, keepdims=False)
    other = lax.dynamic_index_in_dim(by_core, 1 - core, 1, keepdims=False)
    chip_merged = merge([mine, lax.ppermute(other, "ctx", core_pairs(shards))], sums_width)
    parts = [lax.dynamic_index_in_dim(chip_merged, chip, 0, keepdims=False)]
    for step in range(1, chips):
        send = lax.dynamic_index_in_dim(chip_merged, (chip + step) % chips, 0, keepdims=False)
        parts.append(lax.ppermute(send, "ctx", shift_pairs(shards, step)))
    return merge(parts, sums_width)


def body(
    question_hidden,
    recomp_hidden,
    norm_gain,
    w_query,
    w_keyval,
    pool_codes,
    pool_scales,
    block_owner,
    block_slot,
    recomp_pos,
):
    shards = lax.axis_size("ctx")
    own_index = lax.axis_index("ctx")
    q_rows = question_hidden.shape[0]
    r_rows = recomp_hidden.shape[0]
    row_count = q_rows + r_rows
    kv_width = w_keyval.shape[2]
    kv_heads = kv_width // HD
    q_width = w_query.shape[1]
    heads = q_width // HD
    group_size = q_width // kv_width
    score_scale = HD ** (-0.5)

    owners = block_owner[:, 0].reshape(shards, -1)
    per_dev = owners.shape[1]
    slot_table = block_slot.reshape(shards, per_dev)
    capacity = max(2, 2 * per_dev // shards)
    positions = jnp.arange(per_dev)
    earlier_mask = positions[None, :] < positions[:, None]
    same_owner = owners[:, :, None] == owners[:, None, :]
    order_rank = jnp.sum((same_owner & earlier_mask[None]).astype(jnp.int32), axis=2)
    slot_ids = jnp.arange(capacity)
    chosen = (owners == own_index)[:, :, None] & (order_rank[:, :, None] == slot_ids[None, None, :])
    send_slot = jnp.sum(jnp.where(chosen, slot_table[:, :, None], 0), axis=1).reshape(-1)
    block_len = pool_codes.shape[2]
    send_codes = jnp.take(pool_codes, send_slot, axis=0)
    send_scales = jnp.take(pool_scales, send_slot, axis=0)
    send_blocks = (
        send_codes.astype(jnp.float32).reshape(shards * capacity, 2, block_len, kv_heads, HD)
        * send_scales.astype(jnp.float32)[:, :, None, :, None]
    ).astype(jnp.bfloat16).reshape((shards, capacity, 2, block_len, kv_width))
    got_blocks = lax.all_to_all(send_blocks, "ctx", split_axis=0, concat_axis=0, tiled=True)
    ctx_dev = per_dev * block_len
    slot_valid = jnp.any(chosen, axis=1)
    slot_block = jnp.sum(jnp.where(chosen, positions[None, :, None], 0), axis=1)
    slot_base = jnp.arange(shards)[:, None] * ctx_dev + slot_block * block_len
    slot_pos = jnp.where(
        slot_valid[:, :, None], slot_base[:, :, None] + jnp.arange(block_len), -1
    ).reshape(-1)

    normed = jnp.concatenate(
        [rms_rows(question_hidden, norm_gain), rms_rows(recomp_hidden, norm_gain)], axis=0
    )
    pieces = lax.all_to_all(normed, "ctx", split_axis=1, concat_axis=0, tiled=True)
    width_part = pieces.shape[1]
    arranged = pieces.reshape(shards, row_count, width_part)
    question_part = arranged[:, :q_rows, :].reshape(shards * q_rows, width_part)
    kv_weight = w_keyval.reshape(w_keyval.shape[0], 2 * kv_width)
    query_part = jnp.dot(question_part, w_query, preferred_element_type=jnp.float32)
    kv_part = jnp.dot(pieces, kv_weight, preferred_element_type=jnp.float32)

    q_size = q_rows * q_width
    partials = jnp.concatenate(
        [query_part.reshape(shards, q_size), kv_part.reshape(shards, row_count * 2 * kv_width)],
        axis=1,
    )
    gathered = hier_reduce_gather(partials, shards, own_index)
    summed = lax.dynamic_index_in_dim(gathered, own_index, 0, keepdims=False)
    every_query = gathered[:, :q_size].reshape(shards * q_rows, q_width)
    every_kv = gathered[:, q_size:].reshape(shards, row_count, 2, kv_width)
    question_kv = summed[q_size:].reshape(row_count, 2, kv_width)[:q_rows]
    recomp_kv = every_kv[:, q_rows:].reshape(shards * r_rows, 2, kv_width)

    own_owner = lax.dynamic_index_in_dim(owners, own_index, 0, keepdims=False)
    own_rank = lax.dynamic_index_in_dim(order_rank, own_index, 0, keepdims=False)
    flat_index = own_owner * capacity + own_rank
    block_rows = jnp.take(
        got_blocks.reshape((shards * capacity, 2, block_len, kv_width)), flat_index, axis=0
    )
    cached = jnp.transpose(block_rows, (1, 0, 2, 3)).reshape(2, ctx_dev, kv_width)

    local_pos = recomp_pos - own_index * ctx_dev
    match = local_pos[None, :] == jnp.arange(ctx_dev)[:, None]
    hit = jnp.any(match, axis=1)
    one_hot = match.astype(jnp.bfloat16)
    placed = jnp.einsum(
        "pi,ick->cpk", one_hot, recomp_kv, preferred_element_type=jnp.float32
    ).astype(jnp.bfloat16)
    kv_cache = jnp.where(hit[None, :, None], placed, cached)

    slot_count = slot_pos.shape[0]
    own_blocks = jnp.transpose(send_blocks, (2, 0, 1, 3, 4)).reshape(2, slot_count, kv_width)
    owner_match = recomp_pos[None, :] == slot_pos[:, None]
    owner_hit = jnp.any(owner_match, axis=1)
    owner_placed = jnp.einsum(
        "pi,ick->cpk", owner_match.astype(jnp.bfloat16), recomp_kv, preferred_element_type=jnp.float32
    ).astype(jnp.bfloat16)
    owner_kv = jnp.where(owner_hit[None, :, None], owner_placed, own_blocks)
    ctx_bias = jnp.where(slot_pos >= 0, 0.0, neg_large).astype(jnp.float32)[None, :]
    key_rank = (own_index * q_rows + jnp.arange(q_rows)).astype(jnp.int32)[None, :]

    part_sums, part_max, part_total = attend(
        every_query,
        owner_kv[0],
        question_kv[:, 0],
        owner_kv[1],
        question_kv[:, 1],
        ctx_bias,
        key_rank,
        group_size,
        score_scale,
    )

    def by_token(value):
        return jnp.transpose(value[:, :, 0]).reshape(shards, q_rows, heads)

    sent = jnp.concatenate(
        [part_sums.reshape(shards, q_rows, q_width), by_token(part_max), by_token(part_total)],
        axis=2,
    )
    got = hier_combine(sent, shards, own_index, q_width)
    weighted = got[:, :q_width].reshape(q_rows, heads, HD)
    row_total = got[:, q_width + heads :]
    attended = (weighted / row_total[..., None]).reshape(q_rows, q_width).astype(jnp.bfloat16)
    return (attended, kv_cache)


def solution(mesh):
    placed = (
        P(("groups", "ctx"), None),
        P(("groups", "ctx"), None),
        P(),
        P("ctx", "tp"),
        P("ctx", None, "tp"),
        P(("groups", "ctx"), None, None, "tp"),
        P(("groups", "ctx"), None, "tp"),
        P("groups", None),
        P("groups"),
        P("groups"),
    )
    return jax.shard_map(
        body,
        mesh=mesh,
        in_specs=placed,
        out_specs=(P(("groups", "ctx"), "tp"), P(None, ("groups", "ctx"), "tp")),
        check_vma=False,
    )
```

```python
import functools

import jax
import jax.numpy as jnp
from jax import lax
from jax.experimental import pallas as pl
from jax.sharding import PartitionSpec as P

HD = 128


norm_eps = 1e-05
neg_large = -1e30


def rms_rows(hidden, norm_gain):
    floats = hidden.astype(jnp.float32)
    factor = lax.rsqrt(jnp.mean(floats * floats, axis=-1, keepdims=True) + norm_eps)
    return (floats * factor * norm_gain.astype(jnp.float32)).astype(jnp.bfloat16)


def attn_kernel(
    bias_ref, rank_ref, q_ref, kc_ref, kq_ref, vc_ref, vq_ref, o_ref, m_ref, l_ref, *, score_scale
):
    tq = q_ref.shape[0]
    first = pl.program_id(0) * tq
    dims = (((1,), (1,)), ((), ()))
    queries = q_ref[...]
    slots, block_len, width = kc_ref.shape
    ctx_keys = kc_ref[...].reshape(slots * block_len, width)
    ctx_vals = vc_ref[...].reshape(slots * block_len, width)
    ctx_scores = (
        lax.dot_general(queries, ctx_keys, dims, preferred_element_type=jnp.float32)
        * score_scale
        + bias_ref[...]
    )
    own_scores = (
        lax.dot_general(queries, kq_ref[...], dims, preferred_element_type=jnp.float32)
        * score_scale
    )
    token = first + lax.broadcasted_iota(jnp.int32, own_scores.shape, 0)
    shown = rank_ref[...] <= token
    own_masked = jnp.where(shown, own_scores, neg_large)
    row_max = jnp.maximum(
        jnp.max(ctx_scores, axis=1, keepdims=True), jnp.max(own_masked, axis=1, keepdims=True)
    )
    ctx_weights = jnp.exp(ctx_scores - row_max)
    own_weights = jnp.where(shown, jnp.exp(own_masked - row_max), 0.0)
    m_ref[...] = row_max
    l_ref[...] = jnp.sum(ctx_weights, axis=1, keepdims=True) + jnp.sum(
        own_weights, axis=1, keepdims=True
    )
    o_ref[...] = jnp.dot(
        ctx_weights.astype(jnp.bfloat16), ctx_vals, preferred_element_type=jnp.float32
    ) + jnp.dot(own_weights.astype(jnp.bfloat16), vq_ref[...], preferred_element_type=jnp.float32)


def attend(queries, ctx_blocks, own_keys, own_vals, ctx_bias, key_rank, group_size, score_scale):
    tokens, q_width = queries.shape
    slots, double_len, _ = ctx_blocks.shape
    block_len = double_len // 2
    ctx_count = slots * block_len
    own_count = own_keys.shape[0]
    heads = q_width // HD
    tq = min(tokens, 128)
    grid = (tokens // tq, heads)
    return pl.pallas_call(
        functools.partial(attn_kernel, score_scale=score_scale),
        grid=grid,
        in_specs=[
            pl.BlockSpec((1, ctx_count), lambda i, n: (0, 0)),
            pl.BlockSpec((1, own_count), lambda i, n: (0, 0)),
            pl.BlockSpec((tq, HD), lambda i, n: (i, n)),
            pl.BlockSpec((slots, block_len, HD), lambda i, n: (0, 0, n // group_size)),
            pl.BlockSpec((own_count, HD), lambda i, n: (0, n // group_size)),
            pl.BlockSpec((slots, block_len, HD), lambda i, n: (0, 1, n // group_size)),
            pl.BlockSpec((own_count, HD), lambda i, n: (0, n // group_size)),
        ],
        out_specs=[
            pl.BlockSpec((tq, HD), lambda i, n: (i, n)),
            pl.BlockSpec((None, tq, 1), lambda i, n: (n, i, 0)),
            pl.BlockSpec((None, tq, 1), lambda i, n: (n, i, 0)),
        ],
        out_shape=[
            jax.ShapeDtypeStruct((tokens, q_width), jnp.float32),
            jax.ShapeDtypeStruct((heads, tokens, 1), jnp.float32),
            jax.ShapeDtypeStruct((heads, tokens, 1), jnp.float32),
        ],
    )(ctx_bias, key_rank, queries, ctx_blocks, own_keys, ctx_blocks, own_vals)


def shift_pairs(shards, step):
    chips = shards // 2
    return [(i, ((i // 2 + step) % chips) * 2 + i % 2) for i in range(shards)]


def core_pairs(shards):
    return [(i, i ^ 1) for i in range(shards)]


def pick_core(pair, core):
    return jnp.take(pair, jnp.arange(2) ^ core, axis=1)


def hier_reduce_gather(partials, shards, own_index):
    chips = shards // 2
    core = own_index % 2
    chip = own_index // 2
    by_core = partials.reshape(chips, 2, -1)
    mine = lax.dynamic_index_in_dim(by_core, core, 1, keepdims=False)
    other = lax.dynamic_index_in_dim(by_core, 1 - core, 1, keepdims=False)
    chip_sum = mine + lax.ppermute(other, "ctx", core_pairs(shards))
    total = lax.dynamic_index_in_dim(chip_sum, chip, 0, keepdims=False)
    for step in range(1, chips):
        send = lax.dynamic_index_in_dim(chip_sum, (chip + step) % chips, 0, keepdims=False)
        total = total + lax.ppermute(send, "ctx", shift_pairs(shards, step))
    rounded = total.astype(jnp.bfloat16)
    got = [rounded] + [
        lax.ppermute(rounded, "ctx", shift_pairs(shards, step)) for step in range(1, chips)
    ]
    by_shift = jnp.stack(got)
    by_chip = jnp.take(by_shift, (chip - jnp.arange(chips)) % chips, axis=0)
    pair = jnp.stack([by_chip, lax.ppermute(by_chip, "ctx", core_pairs(shards))], axis=1)
    return pick_core(pair, core).reshape(shards, -1)


def merge(parts, sums_width):
    sums = [p[..., :sums_width] for p in parts]
    maxes = [p[..., sums_width:sums_width + (p.shape[-1] - sums_width) // 2] for p in parts]
    totals = [p[..., sums_width + (p.shape[-1] - sums_width) // 2:] for p in parts]
    best = maxes[0]
    for m in maxes[1:]:
        best = jnp.maximum(best, m)
    factors = [jnp.exp(m - best) for m in maxes]
    heads = best.shape[-1]
    lead = sums[0].shape[:-1]
    out_sum = sum(
        s.reshape(lead + (heads, HD)) * f[..., None] for s, f in zip(sums, factors)
    ).reshape(lead + (sums_width,))
    out_total = sum(t * f for t, f in zip(totals, factors))
    return jnp.concatenate([out_sum, best, out_total], axis=-1)


def hier_combine(sent, shards, own_index, sums_width):
    chips = shards // 2
    core = own_index % 2
    chip = own_index // 2
    by_core = sent.reshape((chips, 2) + sent.shape[1:])
    mine = lax.dynamic_index_in_dim(by_core, core, 1, keepdims=False)
    other = lax.dynamic_index_in_dim(by_core, 1 - core, 1, keepdims=False)
    chip_merged = merge([mine, lax.ppermute(other, "ctx", core_pairs(shards))], sums_width)
    parts = [lax.dynamic_index_in_dim(chip_merged, chip, 0, keepdims=False)]
    for step in range(1, chips):
        send = lax.dynamic_index_in_dim(chip_merged, (chip + step) % chips, 0, keepdims=False)
        parts.append(lax.ppermute(send, "ctx", shift_pairs(shards, step)))
    return merge(parts, sums_width)


def body(
    question_hidden,
    recomp_hidden,
    norm_gain,
    w_query,
    w_keyval,
    pool_codes,
    pool_scales,
    block_owner,
    block_slot,
    recomp_pos,
):
    shards = lax.axis_size("ctx")
    own_index = lax.axis_index("ctx")
    q_rows = question_hidden.shape[0]
    r_rows = recomp_hidden.shape[0]
    row_count = q_rows + r_rows
    kv_width = w_keyval.shape[2]
    kv_heads = kv_width // HD
    q_width = w_query.shape[1]
    heads = q_width // HD
    group_size = q_width // kv_width
    score_scale = HD ** (-0.5)

    owners = block_owner[:, 0].reshape(shards, -1)
    per_dev = owners.shape[1]
    slot_table = block_slot.reshape(shards, per_dev)
    capacity = max(2, 2 * per_dev // shards)
    positions = jnp.arange(per_dev)
    earlier_mask = positions[None, :] < positions[:, None]
    same_owner = owners[:, :, None] == owners[:, None, :]
    order_rank = jnp.sum((same_owner & earlier_mask[None]).astype(jnp.int32), axis=2)
    slot_ids = jnp.arange(capacity)
    chosen = (owners == own_index)[:, :, None] & (order_rank[:, :, None] == slot_ids[None, None, :])
    send_slot = jnp.sum(jnp.where(chosen, slot_table[:, :, None], 0), axis=1).reshape(-1)
    block_len = pool_codes.shape[2]
    send_codes = jnp.take(pool_codes, send_slot, axis=0)
    send_scales = jnp.take(pool_scales, send_slot, axis=0)
    send_blocks = (
        send_codes.astype(jnp.float32).reshape(shards * capacity, 2, block_len, kv_heads, HD)
        * send_scales.astype(jnp.float32)[:, :, None, :, None]
    ).astype(jnp.bfloat16).reshape((shards, capacity, 2, block_len, kv_width))
    got_blocks = lax.all_to_all(send_blocks, "ctx", split_axis=0, concat_axis=0, tiled=True)
    ctx_dev = per_dev * block_len
    slot_valid = jnp.any(chosen, axis=1)
    slot_block = jnp.sum(jnp.where(chosen, positions[None, :, None], 0), axis=1)
    slot_base = jnp.arange(shards)[:, None] * ctx_dev + slot_block * block_len
    slot_pos = jnp.where(
        slot_valid[:, :, None], slot_base[:, :, None] + jnp.arange(block_len), -1
    ).reshape(-1)

    normed = jnp.concatenate(
        [rms_rows(question_hidden, norm_gain), rms_rows(recomp_hidden, norm_gain)], axis=0
    )
    pieces = lax.all_to_all(normed, "ctx", split_axis=1, concat_axis=0, tiled=True)
    width_part = pieces.shape[1]
    arranged = pieces.reshape(shards, row_count, width_part)
    question_part = arranged[:, :q_rows, :].reshape(shards * q_rows, width_part)
    kv_weight = w_keyval.reshape(w_keyval.shape[0], 2 * kv_width)
    query_part = jnp.dot(question_part, w_query, preferred_element_type=jnp.float32)
    kv_part = jnp.dot(pieces, kv_weight, preferred_element_type=jnp.float32)

    q_size = q_rows * q_width
    partials = jnp.concatenate(
        [query_part.reshape(shards, q_size), kv_part.reshape(shards, row_count * 2 * kv_width)],
        axis=1,
    )
    gathered = hier_reduce_gather(partials, shards, own_index)
    summed = lax.dynamic_index_in_dim(gathered, own_index, 0, keepdims=False)
    every_query = gathered[:, :q_size].reshape(shards * q_rows, q_width)
    every_kv = gathered[:, q_size:].reshape(shards, row_count, 2, kv_width)
    recomp_kv = every_kv[:, q_rows:].reshape(shards * r_rows, 2, kv_width)

    own_owner = lax.dynamic_index_in_dim(owners, own_index, 0, keepdims=False)
    own_rank = lax.dynamic_index_in_dim(order_rank, own_index, 0, keepdims=False)
    flat_index = own_owner * capacity + own_rank
    block_rows = jnp.take(
        got_blocks.reshape((shards * capacity, 2, block_len, kv_width)), flat_index, axis=0
    )
    cached = jnp.transpose(block_rows, (1, 0, 2, 3)).reshape(2, ctx_dev, kv_width)

    local_pos = recomp_pos - own_index * ctx_dev
    match = local_pos[None, :] == jnp.arange(ctx_dev)[:, None]
    hit = jnp.any(match, axis=1)
    one_hot = match.astype(jnp.bfloat16)
    placed = jnp.einsum(
        "pi,ick->cpk", one_hot, recomp_kv, preferred_element_type=jnp.float32
    ).astype(jnp.bfloat16)
    kv_cache = jnp.where(hit[None, :, None], placed, cached)

    replaced = jnp.any(recomp_pos[None, :] == slot_pos[:, None], axis=1)
    ctx_bias = jnp.where((slot_pos >= 0) & ~replaced, 0.0, neg_large).astype(jnp.float32)[None, :]
    own_kv = summed[q_size:].reshape(row_count, 2, kv_width)
    own_row = jnp.arange(row_count)
    key_rank = jnp.where(own_row < q_rows, own_index * q_rows + own_row, -1).astype(jnp.int32)[None, :]

    part_sums, part_max, part_total = attend(
        every_query,
        send_blocks.reshape(shards * capacity, 2 * block_len, kv_width),
        own_kv[:, 0],
        own_kv[:, 1],
        ctx_bias,
        key_rank,
        group_size,
        score_scale,
    )

    def by_token(value):
        return jnp.transpose(value[:, :, 0]).reshape(shards, q_rows, heads)

    sent = jnp.concatenate(
        [part_sums.reshape(shards, q_rows, q_width), by_token(part_max), by_token(part_total)],
        axis=2,
    )
    got = hier_combine(sent, shards, own_index, q_width)
    weighted = got[:, :q_width].reshape(q_rows, heads, HD)
    row_total = got[:, q_width + heads :]
    attended = (weighted / row_total[..., None]).reshape(q_rows, q_width).astype(jnp.bfloat16)
    return (attended, kv_cache)


def solution(mesh):
    placed = (
        P(("groups", "ctx"), None),
        P(("groups", "ctx"), None),
        P(),
        P("ctx", "tp"),
        P("ctx", None, "tp"),
        P(("groups", "ctx"), None, None, "tp"),
        P(("groups", "ctx"), None, "tp"),
        P("groups", None),
        P("groups"),
        P("groups"),
    )
    return jax.shard_map(
        body,
        mesh=mesh,
        in_specs=placed,
        out_specs=(P(("groups", "ctx"), "tp"), P(None, ("groups", "ctx"), "tp")),
        check_vma=False,
    )
```

```python
import functools

import jax
import jax.numpy as jnp
from jax import lax
from jax.experimental import pallas as pl
from jax.sharding import PartitionSpec as P

HD = 128


norm_eps = 1e-05
neg_large = -1e30


def rms_rows(hidden, norm_gain):
    floats = hidden.astype(jnp.float32)
    factor = lax.rsqrt(jnp.mean(floats * floats, axis=-1, keepdims=True) + norm_eps)
    return (floats * factor * norm_gain.astype(jnp.float32)).astype(jnp.bfloat16)


def attn_kernel(
    bias_ref, rank_ref, q_ref, kc_ref, kq_ref, vc_ref, vq_ref, o_ref, m_ref, l_ref, *, score_scale
):
    tq = q_ref.shape[0]
    first = pl.program_id(0) * tq
    dims = (((1,), (1,)), ((), ()))
    queries = q_ref[...]
    slots, block_len, width = kc_ref.shape
    ctx_keys = kc_ref[...].reshape(slots * block_len, width)
    ctx_vals = vc_ref[...].reshape(slots * block_len, width)
    ctx_scores = (
        lax.dot_general(queries, ctx_keys, dims, preferred_element_type=jnp.float32)
        * score_scale
        + bias_ref[...]
    )
    own_scores = (
        lax.dot_general(queries, kq_ref[...], dims, preferred_element_type=jnp.float32)
        * score_scale
    )
    token = first + lax.broadcasted_iota(jnp.int32, own_scores.shape, 0)
    shown = rank_ref[...] <= token
    own_masked = jnp.where(shown, own_scores, neg_large)
    row_max = jnp.maximum(
        jnp.max(ctx_scores, axis=1, keepdims=True), jnp.max(own_masked, axis=1, keepdims=True)
    )
    ctx_weights = jnp.exp(ctx_scores - row_max)
    own_weights = jnp.where(shown, jnp.exp(own_masked - row_max), 0.0)
    m_ref[...] = row_max
    l_ref[...] = jnp.sum(ctx_weights, axis=1, keepdims=True) + jnp.sum(
        own_weights, axis=1, keepdims=True
    )
    o_ref[...] = jnp.dot(
        ctx_weights.astype(jnp.bfloat16), ctx_vals, preferred_element_type=jnp.float32
    ) + jnp.dot(own_weights.astype(jnp.bfloat16), vq_ref[...], preferred_element_type=jnp.float32)


def attend(queries, ctx_blocks, own_keys, own_vals, ctx_bias, key_rank, group_size, score_scale):
    tokens, q_width = queries.shape
    slots, double_len, _ = ctx_blocks.shape
    block_len = double_len // 2
    ctx_count = slots * block_len
    own_count = own_keys.shape[0]
    heads = q_width // HD
    tq = min(tokens, 128)
    grid = (tokens // tq, heads)
    return pl.pallas_call(
        functools.partial(attn_kernel, score_scale=score_scale),
        grid=grid,
        in_specs=[
            pl.BlockSpec((1, ctx_count), lambda i, n: (0, 0)),
            pl.BlockSpec((1, own_count), lambda i, n: (0, 0)),
            pl.BlockSpec((tq, HD), lambda i, n: (i, n)),
            pl.BlockSpec((slots, block_len, HD), lambda i, n: (0, 0, n // group_size)),
            pl.BlockSpec((own_count, HD), lambda i, n: (0, n // group_size)),
            pl.BlockSpec((slots, block_len, HD), lambda i, n: (0, 1, n // group_size)),
            pl.BlockSpec((own_count, HD), lambda i, n: (0, n // group_size)),
        ],
        out_specs=[
            pl.BlockSpec((tq, HD), lambda i, n: (i, n)),
            pl.BlockSpec((None, tq, 1), lambda i, n: (n, i, 0)),
            pl.BlockSpec((None, tq, 1), lambda i, n: (n, i, 0)),
        ],
        out_shape=[
            jax.ShapeDtypeStruct((tokens, q_width), jnp.float32),
            jax.ShapeDtypeStruct((heads, tokens, 1), jnp.float32),
            jax.ShapeDtypeStruct((heads, tokens, 1), jnp.float32),
        ],
    )(ctx_bias, key_rank, queries, ctx_blocks, own_keys, ctx_blocks, own_vals)


def shift_pairs(shards, step):
    chips = shards // 2
    return [(i, ((i // 2 + step) % chips) * 2 + i % 2) for i in range(shards)]


def core_pairs(shards):
    return [(i, i ^ 1) for i in range(shards)]


def pick_core(pair, core):
    return jnp.take(pair, jnp.arange(2) ^ core, axis=1)


def hier_reduce_gather(partials, shards, own_index):
    chips = shards // 2
    core = own_index % 2
    chip = own_index // 2
    by_core = partials.reshape(chips, 2, -1)
    mine = lax.dynamic_index_in_dim(by_core, core, 1, keepdims=False)
    other = lax.dynamic_index_in_dim(by_core, 1 - core, 1, keepdims=False)
    chip_sum = mine + lax.ppermute(other, "ctx", core_pairs(shards))
    total = lax.dynamic_index_in_dim(chip_sum, chip, 0, keepdims=False)
    for step in range(1, chips):
        send = lax.dynamic_index_in_dim(chip_sum, (chip + step) % chips, 0, keepdims=False)
        total = total + lax.ppermute(send, "ctx", shift_pairs(shards, step))
    rounded = total.astype(jnp.bfloat16)
    got = [rounded] + [
        lax.ppermute(rounded, "ctx", shift_pairs(shards, step)) for step in range(1, chips)
    ]
    by_shift = jnp.stack(got)
    by_chip = jnp.take(by_shift, (chip - jnp.arange(chips)) % chips, axis=0)
    pair = jnp.stack([by_chip, lax.ppermute(by_chip, "ctx", core_pairs(shards))], axis=1)
    return pick_core(pair, core).reshape(shards, -1)


def merge(parts, sums_width):
    sums = [p[..., :sums_width] for p in parts]
    maxes = [p[..., sums_width:sums_width + (p.shape[-1] - sums_width) // 2] for p in parts]
    totals = [p[..., sums_width + (p.shape[-1] - sums_width) // 2:] for p in parts]
    best = maxes[0]
    for m in maxes[1:]:
        best = jnp.maximum(best, m)
    factors = [jnp.exp(m - best) for m in maxes]
    heads = best.shape[-1]
    lead = sums[0].shape[:-1]
    out_sum = sum(
        s.reshape(lead + (heads, HD)) * f[..., None] for s, f in zip(sums, factors)
    ).reshape(lead + (sums_width,))
    out_total = sum(t * f for t, f in zip(totals, factors))
    return jnp.concatenate([out_sum, best, out_total], axis=-1)


def hier_combine(sent, shards, own_index, sums_width):
    chips = shards // 2
    core = own_index % 2
    chip = own_index // 2
    by_core = sent.reshape((chips, 2) + sent.shape[1:])
    mine = lax.dynamic_index_in_dim(by_core, core, 1, keepdims=False)
    other = lax.dynamic_index_in_dim(by_core, 1 - core, 1, keepdims=False)
    chip_merged = merge([mine, lax.ppermute(other, "ctx", core_pairs(shards))], sums_width)
    parts = [lax.dynamic_index_in_dim(chip_merged, chip, 0, keepdims=False)]
    for step in range(1, chips):
        send = lax.dynamic_index_in_dim(chip_merged, (chip + step) % chips, 0, keepdims=False)
        parts.append(lax.ppermute(send, "ctx", shift_pairs(shards, step)))
    return merge(parts, sums_width)


def body(
    question_hidden,
    recomp_hidden,
    norm_gain,
    w_query,
    w_keyval,
    pool_codes,
    pool_scales,
    block_owner,
    block_slot,
    recomp_pos,
):
    shards = lax.axis_size("ctx")
    own_index = lax.axis_index("ctx")
    q_rows = question_hidden.shape[0]
    r_rows = recomp_hidden.shape[0]
    row_count = q_rows + r_rows
    kv_width = w_keyval.shape[2]
    kv_heads = kv_width // HD
    q_width = w_query.shape[1]
    heads = q_width // HD
    group_size = q_width // kv_width
    score_scale = HD ** (-0.5)

    owners = block_owner[:, 0].reshape(shards, -1)
    per_dev = owners.shape[1]
    slot_table = block_slot.reshape(shards, per_dev)
    capacity = max(2, 2 * per_dev // shards)
    positions = jnp.arange(per_dev)
    earlier_mask = positions[None, :] < positions[:, None]
    same_owner = owners[:, :, None] == owners[:, None, :]
    order_rank = jnp.sum((same_owner & earlier_mask[None]).astype(jnp.int32), axis=2)
    slot_ids = jnp.arange(capacity)
    chosen = (owners == own_index)[:, :, None] & (order_rank[:, :, None] == slot_ids[None, None, :])
    send_slot = jnp.sum(jnp.where(chosen, slot_table[:, :, None], 0), axis=1).reshape(-1)
    block_len = pool_codes.shape[2]
    send_codes = jnp.take(pool_codes, send_slot, axis=0)
    send_scales = jnp.take(pool_scales, send_slot, axis=0)
    send_blocks = (
        send_codes.astype(jnp.float32).reshape(shards * capacity, 2, block_len, kv_heads, HD)
        * send_scales.astype(jnp.float32)[:, :, None, :, None]
    ).astype(jnp.bfloat16).reshape((shards, capacity, 2, block_len, kv_width))
    send_blocks = lax.optimization_barrier(send_blocks)
    got_blocks = lax.all_to_all(send_blocks, "ctx", split_axis=0, concat_axis=0, tiled=True)
    ctx_dev = per_dev * block_len
    slot_valid = jnp.any(chosen, axis=1)
    slot_block = jnp.sum(jnp.where(chosen, positions[None, :, None], 0), axis=1)
    slot_base = jnp.arange(shards)[:, None] * ctx_dev + slot_block * block_len
    slot_pos = jnp.where(
        slot_valid[:, :, None], slot_base[:, :, None] + jnp.arange(block_len), -1
    ).reshape(-1)

    normed = jnp.concatenate(
        [rms_rows(question_hidden, norm_gain), rms_rows(recomp_hidden, norm_gain)], axis=0
    )
    pieces = lax.all_to_all(normed, "ctx", split_axis=1, concat_axis=0, tiled=True)
    width_part = pieces.shape[1]
    arranged = pieces.reshape(shards, row_count, width_part)
    question_part = arranged[:, :q_rows, :].reshape(shards * q_rows, width_part)
    kv_weight = w_keyval.reshape(w_keyval.shape[0], 2 * kv_width)
    query_part = jnp.dot(question_part, w_query, preferred_element_type=jnp.float32)
    kv_part = jnp.dot(pieces, kv_weight, preferred_element_type=jnp.float32)

    q_size = q_rows * q_width
    partials = jnp.concatenate(
        [query_part.reshape(shards, q_size), kv_part.reshape(shards, row_count * 2 * kv_width)],
        axis=1,
    )
    gathered = hier_reduce_gather(partials, shards, own_index)
    summed = lax.dynamic_index_in_dim(gathered, own_index, 0, keepdims=False)
    every_query = gathered[:, :q_size].reshape(shards * q_rows, q_width)
    every_kv = gathered[:, q_size:].reshape(shards, row_count, 2, kv_width)
    recomp_kv = every_kv[:, q_rows:].reshape(shards * r_rows, 2, kv_width)

    own_owner = lax.dynamic_index_in_dim(owners, own_index, 0, keepdims=False)
    own_rank = lax.dynamic_index_in_dim(order_rank, own_index, 0, keepdims=False)
    flat_index = own_owner * capacity + own_rank
    block_rows = jnp.take(
        got_blocks.reshape((shards * capacity, 2, block_len, kv_width)), flat_index, axis=0
    )
    cached = jnp.transpose(block_rows, (1, 0, 2, 3)).reshape(2, ctx_dev, kv_width)

    local_pos = recomp_pos - own_index * ctx_dev
    match = local_pos[None, :] == jnp.arange(ctx_dev)[:, None]
    hit = jnp.any(match, axis=1)
    one_hot = match.astype(jnp.bfloat16)
    placed = jnp.einsum(
        "pi,ick->cpk", one_hot, recomp_kv, preferred_element_type=jnp.float32
    ).astype(jnp.bfloat16)
    kv_cache = jnp.where(hit[None, :, None], placed, cached)

    replaced = jnp.any(recomp_pos[None, :] == slot_pos[:, None], axis=1)
    ctx_bias = jnp.where((slot_pos >= 0) & ~replaced, 0.0, neg_large).astype(jnp.float32)[None, :]
    own_kv = summed[q_size:].reshape(row_count, 2, kv_width)
    own_row = jnp.arange(row_count)
    key_rank = jnp.where(own_row < q_rows, own_index * q_rows + own_row, -1).astype(jnp.int32)[None, :]

    part_sums, part_max, part_total = attend(
        every_query,
        send_blocks.reshape(shards * capacity, 2 * block_len, kv_width),
        own_kv[:, 0],
        own_kv[:, 1],
        ctx_bias,
        key_rank,
        group_size,
        score_scale,
    )

    def by_token(value):
        return jnp.transpose(value[:, :, 0]).reshape(shards, q_rows, heads)

    sent = jnp.concatenate(
        [part_sums.reshape(shards, q_rows, q_width), by_token(part_max), by_token(part_total)],
        axis=2,
    )
    got = hier_combine(sent, shards, own_index, q_width)
    weighted = got[:, :q_width].reshape(q_rows, heads, HD)
    row_total = got[:, q_width + heads :]
    attended = (weighted / row_total[..., None]).reshape(q_rows, q_width).astype(jnp.bfloat16)
    return (attended, kv_cache)


def solution(mesh):
    placed = (
        P(("groups", "ctx"), None),
        P(("groups", "ctx"), None),
        P(),
        P("ctx", "tp"),
        P("ctx", None, "tp"),
        P(("groups", "ctx"), None, None, "tp"),
        P(("groups", "ctx"), None, "tp"),
        P("groups", None),
        P("groups"),
        P("groups"),
    )
    return jax.shard_map(
        body,
        mesh=mesh,
        in_specs=placed,
        out_specs=(P(("groups", "ctx"), "tp"), P(None, ("groups", "ctx"), "tp")),
        check_vma=False,
    )
```

```python
import functools

import jax
import jax.numpy as jnp
from jax import lax
from jax.experimental import pallas as pl
from jax.sharding import PartitionSpec as P


HD = 128


norm_eps = 1e-05
neg_large = -1e30


def rms_rows(hidden, norm_gain):
    floats = hidden.astype(jnp.float32)
    factor = lax.rsqrt(jnp.mean(floats * floats, axis=-1, keepdims=True) + norm_eps)
    return (floats * factor * norm_gain.astype(jnp.float32)).astype(jnp.bfloat16)


def attn_kernel(
    bias_ref, rank_ref, q_ref, kc_ref, kq_ref, vc_ref, vq_ref, o_ref, m_ref, l_ref, *, score_scale
):
    tq = q_ref.shape[0]
    first = pl.program_id(0) * tq
    dims = (((1,), (1,)), ((), ()))
    queries = q_ref[...]
    slots, block_len, width = kc_ref.shape
    ctx_keys = kc_ref[...].reshape(slots * block_len, width)
    ctx_vals = vc_ref[...].reshape(slots * block_len, width)
    ctx_scores = (
        lax.dot_general(queries, ctx_keys, dims, preferred_element_type=jnp.float32)
        * score_scale
        + bias_ref[...]
    )
    own_scores = (
        lax.dot_general(queries, kq_ref[...], dims, preferred_element_type=jnp.float32)
        * score_scale
    )
    token = first + lax.broadcasted_iota(jnp.int32, own_scores.shape, 0)
    shown = rank_ref[...] <= token
    own_masked = jnp.where(shown, own_scores, neg_large)
    row_max = jnp.maximum(
        jnp.max(ctx_scores, axis=1, keepdims=True), jnp.max(own_masked, axis=1, keepdims=True)
    )
    ctx_weights = jnp.exp(ctx_scores - row_max)
    own_weights = jnp.where(shown, jnp.exp(own_masked - row_max), 0.0)
    m_ref[...] = row_max
    l_ref[...] = jnp.sum(ctx_weights, axis=1, keepdims=True) + jnp.sum(
        own_weights, axis=1, keepdims=True
    )
    o_ref[...] = jnp.dot(
        ctx_weights.astype(jnp.bfloat16), ctx_vals, preferred_element_type=jnp.float32
    ) + jnp.dot(own_weights.astype(jnp.bfloat16), vq_ref[...], preferred_element_type=jnp.float32)


def attend(queries, ctx_blocks, own_keys, own_vals, ctx_bias, key_rank, group_size, score_scale):
    tokens, q_width = queries.shape
    slots, double_len, _ = ctx_blocks.shape
    block_len = double_len // 2
    ctx_count = slots * block_len
    own_count = own_keys.shape[0]
    heads = q_width // HD
    tq = min(tokens, 128)
    grid = (tokens // tq, heads)
    return pl.pallas_call(
        functools.partial(attn_kernel, score_scale=score_scale),
        grid=grid,
        in_specs=[
            pl.BlockSpec((1, ctx_count), lambda i, n: (0, 0)),
            pl.BlockSpec((1, own_count), lambda i, n: (0, 0)),
            pl.BlockSpec((tq, HD), lambda i, n: (i, n)),
            pl.BlockSpec((slots, block_len, HD), lambda i, n: (0, 0, n // group_size)),
            pl.BlockSpec((own_count, HD), lambda i, n: (0, n // group_size)),
            pl.BlockSpec((slots, block_len, HD), lambda i, n: (0, 1, n // group_size)),
            pl.BlockSpec((own_count, HD), lambda i, n: (0, n // group_size)),
        ],
        out_specs=[
            pl.BlockSpec((tq, HD), lambda i, n: (i, n)),
            pl.BlockSpec((None, tq, 1), lambda i, n: (n, i, 0)),
            pl.BlockSpec((None, tq, 1), lambda i, n: (n, i, 0)),
        ],
        out_shape=[
            jax.ShapeDtypeStruct((tokens, q_width), jnp.float32),
            jax.ShapeDtypeStruct((heads, tokens, 1), jnp.float32),
            jax.ShapeDtypeStruct((heads, tokens, 1), jnp.float32),
        ],
    )(ctx_bias, key_rank, queries, ctx_blocks, own_keys, ctx_blocks, own_vals)


def shift_pairs(shards, step):
    chips = shards // 2
    return [(i, ((i // 2 + step) % chips) * 2 + i % 2) for i in range(shards)]


def core_pairs(shards):
    return [(i, i ^ 1) for i in range(shards)]


def pick_core(pair, core):
    return jnp.take(pair, jnp.arange(2) ^ core, axis=1)


def hier_reduce_gather(partials, shards, own_index):
    chips = shards // 2
    core = own_index % 2
    chip = own_index // 2
    tree = jax.tree.map

    def split(x):
        return x.reshape((chips, 2) + x.shape[1:])

    by_core = tree(split, partials)
    mine = tree(lambda x: lax.dynamic_index_in_dim(x, core, 1, keepdims=False), by_core)
    other = tree(lambda x: lax.dynamic_index_in_dim(x, 1 - core, 1, keepdims=False), by_core)
    chip_sum = tree(jnp.add, mine, lax.ppermute(other, "ctx", core_pairs(shards)))
    total = tree(lambda x: lax.dynamic_index_in_dim(x, chip, 0, keepdims=False), chip_sum)
    for step in range(1, chips):
        send = tree(
            lambda x: lax.dynamic_index_in_dim(x, (chip + step) % chips, 0, keepdims=False),
            chip_sum,
        )
        total = tree(jnp.add, total, lax.ppermute(send, "ctx", shift_pairs(shards, step)))
    rounded = tree(lambda x: x.astype(jnp.bfloat16), total)
    got = [rounded] + [
        lax.ppermute(rounded, "ctx", shift_pairs(shards, step)) for step in range(1, chips)
    ]
    order = (chip - jnp.arange(chips)) % chips
    by_chip = tree(lambda *xs: jnp.take(jnp.stack(xs), order, axis=0), *got)
    partner = lax.ppermute(by_chip, "ctx", core_pairs(shards))

    def join(x, y):
        pair = pick_core(jnp.stack([x, y], axis=1), core)
        return pair.reshape((shards,) + pair.shape[2:])

    return tree(join, by_chip, partner)


def merge(parts, sums_width):
    sums = [p[..., :sums_width] for p in parts]
    maxes = [p[..., sums_width:sums_width + (p.shape[-1] - sums_width) // 2] for p in parts]
    totals = [p[..., sums_width + (p.shape[-1] - sums_width) // 2:] for p in parts]
    best = maxes[0]
    for m in maxes[1:]:
        best = jnp.maximum(best, m)
    factors = [jnp.exp(m - best) for m in maxes]
    heads = best.shape[-1]
    lead = sums[0].shape[:-1]
    out_sum = sum(
        s.reshape(lead + (heads, HD)) * f[..., None] for s, f in zip(sums, factors)
    ).reshape(lead + (sums_width,))
    out_total = sum(t * f for t, f in zip(totals, factors))
    return jnp.concatenate([out_sum, best, out_total], axis=-1)


def hier_combine(sent, shards, own_index, sums_width):
    chips = shards // 2
    core = own_index % 2
    chip = own_index // 2
    by_core = sent.reshape((chips, 2) + sent.shape[1:])
    mine = lax.dynamic_index_in_dim(by_core, core, 1, keepdims=False)
    other = lax.dynamic_index_in_dim(by_core, 1 - core, 1, keepdims=False)
    chip_merged = merge([mine, lax.ppermute(other, "ctx", core_pairs(shards))], sums_width)
    parts = [lax.dynamic_index_in_dim(chip_merged, chip, 0, keepdims=False)]
    for step in range(1, chips):
        send = lax.dynamic_index_in_dim(chip_merged, (chip + step) % chips, 0, keepdims=False)
        parts.append(lax.ppermute(send, "ctx", shift_pairs(shards, step)))
    return merge(parts, sums_width)


def body(
    question_hidden,
    recomp_hidden,
    norm_gain,
    w_query,
    w_keyval,
    pool_codes,
    pool_scales,
    block_owner,
    block_slot,
    recomp_pos,
):
    shards = lax.axis_size("ctx")
    own_index = lax.axis_index("ctx")
    q_rows = question_hidden.shape[0]
    r_rows = recomp_hidden.shape[0]
    row_count = q_rows + r_rows
    kv_width = w_keyval.shape[2]
    kv_heads = kv_width // HD
    q_width = w_query.shape[1]
    heads = q_width // HD
    group_size = q_width // kv_width
    score_scale = HD ** (-0.5)

    owners = block_owner[:, 0].reshape(shards, -1)
    per_dev = owners.shape[1]
    slot_table = block_slot.reshape(shards, per_dev)
    capacity = max(2, 2 * per_dev // shards)
    positions = jnp.arange(per_dev)
    earlier_mask = positions[None, :] < positions[:, None]
    same_owner = owners[:, :, None] == owners[:, None, :]
    order_rank = jnp.sum((same_owner & earlier_mask[None]).astype(jnp.int32), axis=2)
    slot_ids = jnp.arange(capacity)
    chosen = (owners == own_index)[:, :, None] & (order_rank[:, :, None] == slot_ids[None, None, :])
    send_slot = jnp.sum(jnp.where(chosen, slot_table[:, :, None], 0), axis=1).reshape(-1)
    block_len = pool_codes.shape[2]
    send_codes = jnp.take(pool_codes, send_slot, axis=0)
    send_scales = jnp.take(pool_scales, send_slot, axis=0)
    send_blocks = (
        send_codes.astype(jnp.float32).reshape(shards * capacity, 2, block_len, kv_heads, HD)
        * send_scales.astype(jnp.float32)[:, :, None, :, None]
    ).astype(jnp.bfloat16).reshape((shards, capacity, 2, block_len, kv_width))
    send_blocks = lax.optimization_barrier(send_blocks)
    ctx_dev = per_dev * block_len
    slot_valid = jnp.any(chosen, axis=1)
    slot_block = jnp.sum(jnp.where(chosen, positions[None, :, None], 0), axis=1)
    slot_base = jnp.arange(shards)[:, None] * ctx_dev + slot_block * block_len
    slot_pos = jnp.where(
        slot_valid[:, :, None], slot_base[:, :, None] + jnp.arange(block_len), -1
    ).reshape(-1)

    normed = jnp.concatenate(
        [rms_rows(question_hidden, norm_gain), rms_rows(recomp_hidden, norm_gain)], axis=0
    )
    pieces = lax.all_to_all(normed, "ctx", split_axis=1, concat_axis=0, tiled=True)
    width_part = pieces.shape[1]
    arranged = pieces.reshape(shards, row_count, width_part)
    question_part = arranged[:, :q_rows, :].reshape(shards * q_rows, width_part)
    query_part = jnp.dot(question_part, w_query, preferred_element_type=jnp.float32)
    kv_part = jnp.einsum("tk,kcn->tcn", pieces, w_keyval, preferred_element_type=jnp.float32)

    every_query, every_kv = hier_reduce_gather(
        (
            query_part.reshape(shards, q_rows, q_width),
            kv_part.reshape(shards, row_count, 2, kv_width),
        ),
        shards,
        own_index,
    )
    send_later, every_query, every_kv = lax.optimization_barrier(
        (send_blocks, every_query, every_kv)
    )
    got_blocks = lax.all_to_all(send_later, "ctx", split_axis=0, concat_axis=0, tiled=True)
    every_query = every_query.reshape(shards * q_rows, q_width)
    own_kv = lax.dynamic_index_in_dim(every_kv, own_index, 0, keepdims=False)
    recomp_kv = every_kv[:, q_rows:].reshape(shards * r_rows, 2, kv_width)

    own_owner = lax.dynamic_index_in_dim(owners, own_index, 0, keepdims=False)
    own_rank = lax.dynamic_index_in_dim(order_rank, own_index, 0, keepdims=False)
    flat_index = own_owner * capacity + own_rank
    block_rows = jnp.take(
        got_blocks.reshape((shards * capacity, 2, block_len, kv_width)), flat_index, axis=0
    )
    cached = jnp.transpose(block_rows, (1, 0, 2, 3)).reshape(2, ctx_dev, kv_width)

    local_pos = recomp_pos - own_index * ctx_dev
    match = local_pos[None, :] == jnp.arange(ctx_dev)[:, None]
    hit = jnp.any(match, axis=1)
    one_hot = match.astype(jnp.bfloat16)
    placed = jnp.einsum(
        "pi,ick->cpk", one_hot, recomp_kv, preferred_element_type=jnp.float32
    ).astype(jnp.bfloat16)
    kv_cache = jnp.where(hit[None, :, None], placed, cached)

    replaced = jnp.any(recomp_pos[None, :] == slot_pos[:, None], axis=1)
    ctx_bias = jnp.where((slot_pos >= 0) & ~replaced, 0.0, neg_large).astype(jnp.float32)[None, :]
    own_row = jnp.arange(row_count)
    key_rank = jnp.where(own_row < q_rows, own_index * q_rows + own_row, -1).astype(jnp.int32)[None, :]

    part_sums, part_max, part_total = attend(
        every_query,
        send_blocks.reshape(shards * capacity, 2 * block_len, kv_width),
        own_kv[:, 0],
        own_kv[:, 1],
        ctx_bias,
        key_rank,
        group_size,
        score_scale,
    )

    def by_token(value):
        return jnp.transpose(value[:, :, 0]).reshape(shards, q_rows, heads)

    sent = jnp.concatenate(
        [part_sums.reshape(shards, q_rows, q_width), by_token(part_max), by_token(part_total)],
        axis=2,
    )
    got = hier_combine(sent, shards, own_index, q_width)
    weighted = got[:, :q_width].reshape(q_rows, heads, HD)
    row_total = got[:, q_width + heads :]
    attended = (weighted / row_total[..., None]).reshape(q_rows, q_width).astype(jnp.bfloat16)
    return (attended, kv_cache)


def solution(mesh):
    placed = (
        P(("groups", "ctx"), None),
        P(("groups", "ctx"), None),
        P(),
        P("ctx", "tp"),
        P("ctx", None, "tp"),
        P(("groups", "ctx"), None, None, "tp"),
        P(("groups", "ctx"), None, "tp"),
        P("groups", None),
        P("groups"),
        P("groups"),
    )
    return jax.shard_map(
        body,
        mesh=mesh,
        in_specs=placed,
        out_specs=(P(("groups", "ctx"), "tp"), P(None, ("groups", "ctx"), "tp")),
        check_vma=False,
    )
```

```python
import functools

import jax
import jax.numpy as jnp
from jax import lax
from jax.experimental import pallas as pl
from jax.sharding import PartitionSpec as P


HD = 128


norm_eps = 1e-05
neg_large = -1e30


def rms_rows(hidden, norm_gain):
    floats = hidden.astype(jnp.float32)
    factor = lax.rsqrt(jnp.mean(floats * floats, axis=-1, keepdims=True) + norm_eps)
    return (floats * factor * norm_gain.astype(jnp.float32)).astype(jnp.bfloat16)


def attn_kernel(bias_ref, rank_ref, q_ref, kc_ref, kq_ref, vc_ref, vq_ref, o_ref, m_ref, l_ref, *, score_scale, group):
    slots, block_len, width = kc_ref.shape
    ctx_keys = kc_ref[...].reshape(slots * block_len, width)
    ctx_vals = vc_ref[...].reshape(slots * block_len, width)
    own_keys = kq_ref[...]
    own_vals = vq_ref[...]
    bias = bias_ref[...]
    dims = (((1,), (1,)), ((), ()))
    tq = q_ref.shape[0]
    first = pl.program_id(0) * tq
    token = first + lax.broadcasted_iota(jnp.int32, (tq, own_keys.shape[0]), 0)
    shown = rank_ref[...] <= token
    for g in range(group):
        queries = q_ref[:, g * HD : (g + 1) * HD]
        cs = (
            lax.dot_general(queries, ctx_keys, dims, preferred_element_type=jnp.float32)
            * score_scale
            + bias
        )
        os_ = (
            lax.dot_general(queries, own_keys, dims, preferred_element_type=jnp.float32)
            * score_scale
        )
        om = jnp.where(shown, os_, neg_large)
        mx = jnp.maximum(jnp.max(cs, axis=1, keepdims=True), jnp.max(om, axis=1, keepdims=True))
        cw = jnp.exp(cs - mx)
        ow = jnp.where(shown, jnp.exp(om - mx), 0.0)
        m_ref[g] = mx
        l_ref[g] = jnp.sum(cw, axis=1, keepdims=True) + jnp.sum(ow, axis=1, keepdims=True)
        o_ref[:, g * HD : (g + 1) * HD] = jnp.dot(
            cw.astype(jnp.bfloat16), ctx_vals, preferred_element_type=jnp.float32
        ) + jnp.dot(ow.astype(jnp.bfloat16), own_vals, preferred_element_type=jnp.float32)


def attend(queries, ctx_blocks, own_keys, own_vals, ctx_bias, key_rank, group_size, score_scale):
    tokens, q_width = queries.shape
    slots, double_len, _ = ctx_blocks.shape
    block_len = double_len // 2
    ctx_count = slots * block_len
    own_count = own_keys.shape[0]
    heads = q_width // HD
    kvh = heads // group_size
    tq = min(tokens, 128)
    return pl.pallas_call(
        functools.partial(attn_kernel, score_scale=score_scale, group=group_size),
        grid=(tokens // tq, kvh),
        in_specs=[
            pl.BlockSpec((1, ctx_count), lambda i, h: (0, 0)),
            pl.BlockSpec((1, own_count), lambda i, h: (0, 0)),
            pl.BlockSpec((tq, HD * group_size), lambda i, h: (i, h)),
            pl.BlockSpec((slots, block_len, HD), lambda i, h: (0, 0, h)),
            pl.BlockSpec((own_count, HD), lambda i, h: (0, h)),
            pl.BlockSpec((slots, block_len, HD), lambda i, h: (0, 1, h)),
            pl.BlockSpec((own_count, HD), lambda i, h: (0, h)),
        ],
        out_specs=[
            pl.BlockSpec((tq, HD * group_size), lambda i, h: (i, h)),
            pl.BlockSpec((group_size, tq, 1), lambda i, h: (h, i, 0)),
            pl.BlockSpec((group_size, tq, 1), lambda i, h: (h, i, 0)),
        ],
        out_shape=[
            jax.ShapeDtypeStruct((tokens, q_width), jnp.float32),
            jax.ShapeDtypeStruct((heads, tokens, 1), jnp.float32),
            jax.ShapeDtypeStruct((heads, tokens, 1), jnp.float32),
        ],
    )(ctx_bias, key_rank, queries, ctx_blocks, own_keys, ctx_blocks, own_vals)


def shift_pairs(shards, step):
    chips = shards // 2
    return [(i, ((i // 2 + step) % chips) * 2 + i % 2) for i in range(shards)]


def core_pairs(shards):
    return [(i, i ^ 1) for i in range(shards)]


def pick_core(pair, core):
    return jnp.take(pair, jnp.arange(2) ^ core, axis=1)


def hier_reduce_gather(partials, shards, own_index):
    chips = shards // 2
    core = own_index % 2
    chip = own_index // 2
    tree = jax.tree.map

    def split(x):
        return x.reshape((chips, 2) + x.shape[1:])

    by_core = tree(split, partials)
    mine = tree(lambda x: lax.dynamic_index_in_dim(x, core, 1, keepdims=False), by_core)
    other = tree(lambda x: lax.dynamic_index_in_dim(x, 1 - core, 1, keepdims=False), by_core)
    chip_sum = tree(jnp.add, mine, lax.ppermute(other, "ctx", core_pairs(shards)))
    total = tree(lambda x: lax.dynamic_index_in_dim(x, chip, 0, keepdims=False), chip_sum)
    for step in range(1, chips):
        send = tree(
            lambda x: lax.dynamic_index_in_dim(x, (chip + step) % chips, 0, keepdims=False),
            chip_sum,
        )
        total = tree(jnp.add, total, lax.ppermute(send, "ctx", shift_pairs(shards, step)))
    rounded = tree(lambda x: x.astype(jnp.bfloat16), total)
    got = [rounded] + [
        lax.ppermute(rounded, "ctx", shift_pairs(shards, step)) for step in range(1, chips)
    ]
    order = (chip - jnp.arange(chips)) % chips
    by_chip = tree(lambda *xs: jnp.take(jnp.stack(xs), order, axis=0), *got)
    partner = lax.ppermute(by_chip, "ctx", core_pairs(shards))

    def join(x, y):
        pair = pick_core(jnp.stack([x, y], axis=1), core)
        return pair.reshape((shards,) + pair.shape[2:])

    return tree(join, by_chip, partner)


def merge(parts, sums_width):
    sums = [p[..., :sums_width] for p in parts]
    maxes = [p[..., sums_width:sums_width + (p.shape[-1] - sums_width) // 2] for p in parts]
    totals = [p[..., sums_width + (p.shape[-1] - sums_width) // 2:] for p in parts]
    best = maxes[0]
    for m in maxes[1:]:
        best = jnp.maximum(best, m)
    factors = [jnp.exp(m - best) for m in maxes]
    heads = best.shape[-1]
    lead = sums[0].shape[:-1]
    out_sum = sum(
        s.reshape(lead + (heads, HD)) * f[..., None] for s, f in zip(sums, factors)
    ).reshape(lead + (sums_width,))
    out_total = sum(t * f for t, f in zip(totals, factors))
    return jnp.concatenate([out_sum, best, out_total], axis=-1)


def hier_combine(sent, shards, own_index, sums_width):
    chips = shards // 2
    core = own_index % 2
    chip = own_index // 2
    by_core = sent.reshape((chips, 2) + sent.shape[1:])
    mine = lax.dynamic_index_in_dim(by_core, core, 1, keepdims=False)
    other = lax.dynamic_index_in_dim(by_core, 1 - core, 1, keepdims=False)
    chip_merged = merge([mine, lax.ppermute(other, "ctx", core_pairs(shards))], sums_width)
    parts = [lax.dynamic_index_in_dim(chip_merged, chip, 0, keepdims=False)]
    for step in range(1, chips):
        send = lax.dynamic_index_in_dim(chip_merged, (chip + step) % chips, 0, keepdims=False)
        parts.append(lax.ppermute(send, "ctx", shift_pairs(shards, step)))
    return merge(parts, sums_width)


def body(
    question_hidden,
    recomp_hidden,
    norm_gain,
    w_query,
    w_keyval,
    pool_codes,
    pool_scales,
    block_owner,
    block_slot,
    recomp_pos,
):
    shards = lax.axis_size("ctx")
    own_index = lax.axis_index("ctx")
    q_rows = question_hidden.shape[0]
    r_rows = recomp_hidden.shape[0]
    row_count = q_rows + r_rows
    kv_width = w_keyval.shape[2]
    kv_heads = kv_width // HD
    q_width = w_query.shape[1]
    heads = q_width // HD
    group_size = q_width // kv_width
    score_scale = HD ** (-0.5)

    owners = block_owner[:, 0].reshape(shards, -1)
    per_dev = owners.shape[1]
    slot_table = block_slot.reshape(shards, per_dev)
    capacity = max(2, 2 * per_dev // shards)
    positions = jnp.arange(per_dev)
    earlier_mask = positions[None, :] < positions[:, None]
    same_owner = owners[:, :, None] == owners[:, None, :]
    order_rank = jnp.sum((same_owner & earlier_mask[None]).astype(jnp.int32), axis=2)
    slot_ids = jnp.arange(capacity)
    chosen = (owners == own_index)[:, :, None] & (order_rank[:, :, None] == slot_ids[None, None, :])
    send_slot = jnp.sum(jnp.where(chosen, slot_table[:, :, None], 0), axis=1).reshape(-1)
    block_len = pool_codes.shape[2]
    send_codes = jnp.take(pool_codes, send_slot, axis=0)
    send_scales = jnp.take(pool_scales, send_slot, axis=0)
    send_blocks = (
        send_codes.astype(jnp.float32).reshape(shards * capacity, 2, block_len, kv_heads, HD)
        * send_scales.astype(jnp.float32)[:, :, None, :, None]
    ).astype(jnp.bfloat16).reshape((shards, capacity, 2, block_len, kv_width))
    send_blocks = lax.optimization_barrier(send_blocks)
    ctx_dev = per_dev * block_len
    slot_valid = jnp.any(chosen, axis=1)
    slot_block = jnp.sum(jnp.where(chosen, positions[None, :, None], 0), axis=1)
    slot_base = jnp.arange(shards)[:, None] * ctx_dev + slot_block * block_len
    slot_pos = jnp.where(
        slot_valid[:, :, None], slot_base[:, :, None] + jnp.arange(block_len), -1
    ).reshape(-1)

    normed = jnp.concatenate(
        [rms_rows(question_hidden, norm_gain), rms_rows(recomp_hidden, norm_gain)], axis=0
    )
    pieces = lax.all_to_all(normed, "ctx", split_axis=1, concat_axis=0, tiled=True)
    width_part = pieces.shape[1]
    arranged = pieces.reshape(shards, row_count, width_part)
    question_part = arranged[:, :q_rows, :].reshape(shards * q_rows, width_part)
    query_part = jnp.dot(question_part, w_query, preferred_element_type=jnp.float32)
    kv_part = jnp.einsum("tk,kcn->tcn", pieces, w_keyval, preferred_element_type=jnp.float32)

    every_query, every_kv = hier_reduce_gather(
        (
            query_part.reshape(shards, q_rows, q_width),
            kv_part.reshape(shards, row_count, 2, kv_width),
        ),
        shards,
        own_index,
    )
    send_later, every_query, every_kv = lax.optimization_barrier(
        (send_blocks, every_query, every_kv)
    )
    got_blocks = lax.all_to_all(send_later, "ctx", split_axis=0, concat_axis=0, tiled=True)
    every_query = every_query.reshape(shards * q_rows, q_width)
    own_kv = lax.dynamic_index_in_dim(every_kv, own_index, 0, keepdims=False)
    recomp_kv = every_kv[:, q_rows:].reshape(shards * r_rows, 2, kv_width)

    own_owner = lax.dynamic_index_in_dim(owners, own_index, 0, keepdims=False)
    own_rank = lax.dynamic_index_in_dim(order_rank, own_index, 0, keepdims=False)
    flat_index = own_owner * capacity + own_rank
    block_rows = jnp.take(
        got_blocks.reshape((shards * capacity, 2, block_len, kv_width)), flat_index, axis=0
    )
    cached = jnp.transpose(block_rows, (1, 0, 2, 3)).reshape(2, ctx_dev, kv_width)

    local_pos = recomp_pos - own_index * ctx_dev
    match = local_pos[None, :] == jnp.arange(ctx_dev)[:, None]
    hit = jnp.any(match, axis=1)
    one_hot = match.astype(jnp.bfloat16)
    placed = jnp.einsum(
        "pi,ick->cpk", one_hot, recomp_kv, preferred_element_type=jnp.float32
    ).astype(jnp.bfloat16)
    kv_cache = jnp.where(hit[None, :, None], placed, cached)

    replaced = jnp.any(recomp_pos[None, :] == slot_pos[:, None], axis=1)
    ctx_bias = jnp.where((slot_pos >= 0) & ~replaced, 0.0, neg_large).astype(jnp.float32)[None, :]
    own_row = jnp.arange(row_count)
    key_rank = jnp.where(own_row < q_rows, own_index * q_rows + own_row, -1).astype(jnp.int32)[None, :]

    part_sums, part_max, part_total = attend(
        every_query,
        send_blocks.reshape(shards * capacity, 2 * block_len, kv_width),
        own_kv[:, 0],
        own_kv[:, 1],
        ctx_bias,
        key_rank,
        group_size,
        score_scale,
    )

    def by_token(value):
        return jnp.transpose(value[:, :, 0]).reshape(shards, q_rows, heads)

    sent = jnp.concatenate(
        [part_sums.reshape(shards, q_rows, q_width), by_token(part_max), by_token(part_total)],
        axis=2,
    )
    got = hier_combine(sent, shards, own_index, q_width)
    weighted = got[:, :q_width].reshape(q_rows, heads, HD)
    row_total = got[:, q_width + heads :]
    attended = (weighted / row_total[..., None]).reshape(q_rows, q_width).astype(jnp.bfloat16)
    return (attended, kv_cache)


def solution(mesh):
    placed = (
        P(("groups", "ctx"), None),
        P(("groups", "ctx"), None),
        P(),
        P("ctx", "tp"),
        P("ctx", None, "tp"),
        P(("groups", "ctx"), None, None, "tp"),
        P(("groups", "ctx"), None, "tp"),
        P("groups", None),
        P("groups"),
        P("groups"),
    )
    return jax.shard_map(
        body,
        mesh=mesh,
        in_specs=placed,
        out_specs=(P(("groups", "ctx"), "tp"), P(None, ("groups", "ctx"), "tp")),
        check_vma=False,
    )
```

```python
import functools

import jax
import jax.numpy as jnp
from jax import lax
from jax.experimental import pallas as pl
from jax.sharding import PartitionSpec as P


HD = 128


norm_eps = 1e-05
neg_large = -1e30


def rms_rows(hidden, norm_gain):
    floats = hidden.astype(jnp.float32)
    factor = lax.rsqrt(jnp.mean(floats * floats, axis=-1, keepdims=True) + norm_eps)
    return (floats * factor * norm_gain.astype(jnp.float32)).astype(jnp.bfloat16)


def attn_kernel(bias_ref, rank_ref, q_ref, kc_ref, kq_ref, vc_ref, vq_ref, o_ref, m_ref, l_ref, *, score_scale, group):
    slots, block_len, width = kc_ref.shape
    ctx_keys = kc_ref[...].reshape(slots * block_len, width)
    ctx_vals = vc_ref[...].reshape(slots * block_len, width)
    own_keys = kq_ref[...]
    own_vals = vq_ref[...]
    bias = bias_ref[...]
    dims = (((1,), (1,)), ((), ()))
    tq = q_ref.shape[0]
    first = pl.program_id(0) * tq
    token = first + lax.broadcasted_iota(jnp.int32, (tq, own_keys.shape[0]), 0)
    shown = rank_ref[...] <= token
    for g in range(group):
        queries = q_ref[:, g * HD : (g + 1) * HD]
        cs = (
            lax.dot_general(queries, ctx_keys, dims, preferred_element_type=jnp.float32)
            * score_scale
            + bias
        )
        os_ = (
            lax.dot_general(queries, own_keys, dims, preferred_element_type=jnp.float32)
            * score_scale
        )
        om = jnp.where(shown, os_, neg_large)
        mx = jnp.maximum(jnp.max(cs, axis=1, keepdims=True), jnp.max(om, axis=1, keepdims=True))
        cw = jnp.exp(cs - mx)
        ow = jnp.where(shown, jnp.exp(om - mx), 0.0)
        m_ref[g] = mx
        l_ref[g] = jnp.sum(cw, axis=1, keepdims=True) + jnp.sum(ow, axis=1, keepdims=True)
        o_ref[:, g * HD : (g + 1) * HD] = jnp.dot(
            cw.astype(jnp.bfloat16), ctx_vals, preferred_element_type=jnp.float32
        ) + jnp.dot(ow.astype(jnp.bfloat16), own_vals, preferred_element_type=jnp.float32)


def attend(queries, ctx_blocks, own_keys, own_vals, ctx_bias, key_rank, group_size, score_scale):
    tokens, q_width = queries.shape
    slots, double_len, _ = ctx_blocks.shape
    block_len = double_len // 2
    ctx_count = slots * block_len
    own_count = own_keys.shape[0]
    heads = q_width // HD
    kvh = heads // group_size
    tq = min(tokens, 128)
    return pl.pallas_call(
        functools.partial(attn_kernel, score_scale=score_scale, group=group_size),
        grid=(tokens // tq, kvh),
        in_specs=[
            pl.BlockSpec((1, ctx_count), lambda i, h: (0, 0)),
            pl.BlockSpec((1, own_count), lambda i, h: (0, 0)),
            pl.BlockSpec((tq, HD * group_size), lambda i, h: (i, h)),
            pl.BlockSpec((slots, block_len, HD), lambda i, h: (0, 0, h)),
            pl.BlockSpec((own_count, HD), lambda i, h: (0, h)),
            pl.BlockSpec((slots, block_len, HD), lambda i, h: (0, 1, h)),
            pl.BlockSpec((own_count, HD), lambda i, h: (0, h)),
        ],
        out_specs=[
            pl.BlockSpec((tq, HD * group_size), lambda i, h: (i, h)),
            pl.BlockSpec((group_size, tq, 1), lambda i, h: (h, i, 0)),
            pl.BlockSpec((group_size, tq, 1), lambda i, h: (h, i, 0)),
        ],
        out_shape=[
            jax.ShapeDtypeStruct((tokens, q_width), jnp.float32),
            jax.ShapeDtypeStruct((heads, tokens, 1), jnp.float32),
            jax.ShapeDtypeStruct((heads, tokens, 1), jnp.float32),
        ],
    )(ctx_bias, key_rank, queries, ctx_blocks, own_keys, ctx_blocks, own_vals)


def shift_pairs(shards, step):
    chips = shards // 2
    return [(i, ((i // 2 + step) % chips) * 2 + i % 2) for i in range(shards)]


def core_pairs(shards):
    return [(i, i ^ 1) for i in range(shards)]


def pick_core(pair, core):
    return jnp.take(pair, jnp.arange(2) ^ core, axis=1)


def hier_reduce_gather(partials, shards, own_index):
    chips = shards // 2
    core = own_index % 2
    chip = own_index // 2
    tree = jax.tree.map

    def split(x):
        return x.reshape((chips, 2) + x.shape[1:])

    by_core = tree(split, partials)
    mine = tree(lambda x: lax.dynamic_index_in_dim(x, core, 1, keepdims=False), by_core)
    other = tree(lambda x: lax.dynamic_index_in_dim(x, 1 - core, 1, keepdims=False), by_core)
    chip_sum = tree(jnp.add, mine, lax.ppermute(other, "ctx", core_pairs(shards)))
    total = tree(lambda x: lax.dynamic_index_in_dim(x, chip, 0, keepdims=False), chip_sum)
    for step in range(1, chips):
        send = tree(
            lambda x: lax.dynamic_index_in_dim(x, (chip + step) % chips, 0, keepdims=False),
            chip_sum,
        )
        total = tree(jnp.add, total, lax.ppermute(send, "ctx", shift_pairs(shards, step)))
    rounded = tree(lambda x: x.astype(jnp.bfloat16), total)
    got = [rounded] + [
        lax.ppermute(rounded, "ctx", shift_pairs(shards, step)) for step in range(1, chips)
    ]
    order = (chip - jnp.arange(chips)) % chips
    by_chip = tree(lambda *xs: jnp.take(jnp.stack(xs), order, axis=0), *got)
    partner = lax.ppermute(by_chip, "ctx", core_pairs(shards))

    def join(x, y):
        pair = pick_core(jnp.stack([x, y], axis=1), core)
        return pair.reshape((shards,) + pair.shape[2:])

    return tree(join, by_chip, partner)


def merge(parts, sums_width):
    sums = [p[..., :sums_width] for p in parts]
    maxes = [p[..., sums_width:sums_width + (p.shape[-1] - sums_width) // 2] for p in parts]
    totals = [p[..., sums_width + (p.shape[-1] - sums_width) // 2:] for p in parts]
    best = maxes[0]
    for m in maxes[1:]:
        best = jnp.maximum(best, m)
    factors = [jnp.exp(m - best) for m in maxes]
    heads = best.shape[-1]
    lead = sums[0].shape[:-1]
    out_sum = sum(
        s.reshape(lead + (heads, HD)) * f[..., None] for s, f in zip(sums, factors)
    ).reshape(lead + (sums_width,))
    out_total = sum(t * f for t, f in zip(totals, factors))
    return jnp.concatenate([out_sum, best, out_total], axis=-1)


def hier_combine(sent, shards, own_index, sums_width):
    chips = shards // 2
    core = own_index % 2
    chip = own_index // 2
    by_core = sent.reshape((chips, 2) + sent.shape[1:])
    mine = lax.dynamic_index_in_dim(by_core, core, 1, keepdims=False)
    other = lax.dynamic_index_in_dim(by_core, 1 - core, 1, keepdims=False)
    chip_merged = merge([mine, lax.ppermute(other, "ctx", core_pairs(shards))], sums_width)
    parts = [lax.dynamic_index_in_dim(chip_merged, chip, 0, keepdims=False)]
    for step in range(1, chips):
        send = lax.dynamic_index_in_dim(chip_merged, (chip + step) % chips, 0, keepdims=False)
        parts.append(lax.ppermute(send, "ctx", shift_pairs(shards, step)))
    return merge(parts, sums_width)


def body(
    question_hidden,
    recomp_hidden,
    norm_gain,
    w_query,
    w_keyval,
    pool_codes,
    pool_scales,
    block_owner,
    block_slot,
    recomp_pos,
):
    shards = lax.axis_size("ctx")
    own_index = lax.axis_index("ctx")
    q_rows = question_hidden.shape[0]
    r_rows = recomp_hidden.shape[0]
    row_count = q_rows + r_rows
    kv_width = w_keyval.shape[2]
    kv_heads = kv_width // HD
    q_width = w_query.shape[1]
    heads = q_width // HD
    group_size = q_width // kv_width
    score_scale = HD ** (-0.5)

    owners = block_owner[:, 0].reshape(shards, -1)
    per_dev = owners.shape[1]
    slot_table = block_slot.reshape(shards, per_dev)
    capacity = max(2, 2 * per_dev // shards)
    positions = jnp.arange(per_dev)
    earlier_mask = positions[None, :] < positions[:, None]
    same_owner = owners[:, :, None] == owners[:, None, :]
    order_rank = jnp.sum((same_owner & earlier_mask[None]).astype(jnp.int32), axis=2)
    slot_ids = jnp.arange(capacity)
    chosen = (owners == own_index)[:, :, None] & (order_rank[:, :, None] == slot_ids[None, None, :])
    send_slot = jnp.sum(jnp.where(chosen, slot_table[:, :, None], 0), axis=1).reshape(-1)
    block_len = pool_codes.shape[2]
    send_codes = jnp.take(pool_codes, send_slot, axis=0)
    send_scales = jnp.take(pool_scales, send_slot, axis=0)
    send_blocks = (
        send_codes.astype(jnp.float32).reshape(shards * capacity, 2, block_len, kv_heads, HD)
        * send_scales.astype(jnp.float32)[:, :, None, :, None]
    ).astype(jnp.bfloat16).reshape((shards, capacity, 2, block_len, kv_width))
    send_blocks = lax.optimization_barrier(send_blocks)
    ctx_dev = per_dev * block_len
    slot_valid = jnp.any(chosen, axis=1)
    slot_block = jnp.sum(jnp.where(chosen, positions[None, :, None], 0), axis=1)
    slot_base = jnp.arange(shards)[:, None] * ctx_dev + slot_block * block_len
    slot_pos = jnp.where(
        slot_valid[:, :, None], slot_base[:, :, None] + jnp.arange(block_len), -1
    ).reshape(-1)

    normed = jnp.concatenate(
        [rms_rows(question_hidden, norm_gain), rms_rows(recomp_hidden, norm_gain)], axis=0
    )
    pieces = lax.all_to_all(normed, "ctx", split_axis=1, concat_axis=0, tiled=True)
    width_part = pieces.shape[1]
    arranged = pieces.reshape(shards, row_count, width_part)
    question_part = arranged[:, :q_rows, :].reshape(shards * q_rows, width_part)
    query_part = jnp.dot(question_part, w_query, preferred_element_type=jnp.float32)
    kv_part = jnp.einsum("tk,kcn->tcn", pieces, w_keyval, preferred_element_type=jnp.float32)

    every_query, every_kv = hier_reduce_gather(
        (
            query_part.reshape(shards, q_rows, q_width),
            kv_part.reshape(shards, row_count, 2, kv_width),
        ),
        shards,
        own_index,
    )
    send_later, every_query, every_kv = lax.optimization_barrier(
        (send_blocks, every_query, every_kv)
    )
    got_blocks = lax.all_to_all(send_later, "ctx", split_axis=0, concat_axis=0, tiled=True)
    every_query = every_query.reshape(shards * q_rows, q_width)
    own_kv = lax.dynamic_index_in_dim(every_kv, own_index, 0, keepdims=False)
    recomp_kv = every_kv[:, q_rows:].reshape(shards * r_rows, 2, kv_width)

    own_owner = lax.dynamic_index_in_dim(owners, own_index, 0, keepdims=False)
    own_rank = lax.dynamic_index_in_dim(order_rank, own_index, 0, keepdims=False)
    flat_index = own_owner * capacity + own_rank
    local_pos = recomp_pos - own_index * ctx_dev
    match = local_pos[None, :] == jnp.arange(ctx_dev)[:, None]
    hit = jnp.any(match, axis=1)
    one_hot = match.astype(jnp.bfloat16)
    by_slot = got_blocks.reshape((shards * capacity, 2, block_len, kv_width))
    kv_parts = []
    for c in range(2):
        placed = jnp.dot(
            one_hot, recomp_kv[:, c], preferred_element_type=jnp.float32
        ).astype(jnp.bfloat16)
        cached = jnp.take(by_slot[:, c], flat_index, axis=0).reshape(ctx_dev, kv_width)
        kv_parts.append(jnp.where(hit[:, None], placed, cached))
    kv_cache = jnp.stack(kv_parts)

    replaced = jnp.any(recomp_pos[None, :] == slot_pos[:, None], axis=1)
    ctx_bias = jnp.where((slot_pos >= 0) & ~replaced, 0.0, neg_large).astype(jnp.float32)[None, :]
    own_row = jnp.arange(row_count)
    key_rank = jnp.where(own_row < q_rows, own_index * q_rows + own_row, -1).astype(jnp.int32)[None, :]

    part_sums, part_max, part_total = attend(
        every_query,
        send_blocks.reshape(shards * capacity, 2 * block_len, kv_width),
        own_kv[:, 0],
        own_kv[:, 1],
        ctx_bias,
        key_rank,
        group_size,
        score_scale,
    )

    def by_token(value):
        return jnp.transpose(value[:, :, 0]).reshape(shards, q_rows, heads)

    sent = jnp.concatenate(
        [part_sums.reshape(shards, q_rows, q_width), by_token(part_max), by_token(part_total)],
        axis=2,
    )
    got = hier_combine(sent, shards, own_index, q_width)
    weighted = got[:, :q_width].reshape(q_rows, heads, HD)
    row_total = got[:, q_width + heads :]
    attended = (weighted / row_total[..., None]).reshape(q_rows, q_width).astype(jnp.bfloat16)
    return (attended, kv_cache)


def solution(mesh):
    placed = (
        P(("groups", "ctx"), None),
        P(("groups", "ctx"), None),
        P(),
        P("ctx", "tp"),
        P("ctx", None, "tp"),
        P(("groups", "ctx"), None, None, "tp"),
        P(("groups", "ctx"), None, "tp"),
        P("groups", None),
        P("groups"),
        P("groups"),
    )
    return jax.shard_map(
        body,
        mesh=mesh,
        in_specs=placed,
        out_specs=(P(("groups", "ctx"), "tp"), P(None, ("groups", "ctx"), "tp")),
        check_vma=False,
    )
```

```python
import functools

import jax
import jax.numpy as jnp
from jax import lax
from jax.experimental import pallas as pl
from jax.sharding import PartitionSpec as P


HD = 128


norm_eps = 1e-05
neg_large = -1e30


def rms_rows(hidden, norm_gain):
    floats = hidden.astype(jnp.float32)
    factor = lax.rsqrt(jnp.mean(floats * floats, axis=-1, keepdims=True) + norm_eps)
    return (floats * factor * norm_gain.astype(jnp.float32)).astype(jnp.bfloat16)


def attn_kernel(bias_ref, rank_ref, q_ref, kc_ref, kq_ref, vc_ref, vq_ref, o_ref, m_ref, l_ref, *, score_scale, group):
    slots, block_len, width = kc_ref.shape
    ctx_keys = kc_ref[...].reshape(slots * block_len, width)
    ctx_vals = vc_ref[...].reshape(slots * block_len, width)
    own_keys = kq_ref[...]
    own_vals = vq_ref[...]
    bias = bias_ref[...]
    dims = (((1,), (1,)), ((), ()))
    tq = q_ref.shape[0]
    first = pl.program_id(0) * tq
    token = first + lax.broadcasted_iota(jnp.int32, (tq, own_keys.shape[0]), 0)
    shown = rank_ref[...] <= token
    for g in range(group):
        queries = q_ref[:, g * HD : (g + 1) * HD]
        cs = (
            lax.dot_general(queries, ctx_keys, dims, preferred_element_type=jnp.float32)
            * score_scale
            + bias
        )
        os_ = (
            lax.dot_general(queries, own_keys, dims, preferred_element_type=jnp.float32)
            * score_scale
        )
        om = jnp.where(shown, os_, neg_large)
        mx = jnp.maximum(jnp.max(cs, axis=1, keepdims=True), jnp.max(om, axis=1, keepdims=True))
        cw = jnp.exp(cs - mx)
        ow = jnp.where(shown, jnp.exp(om - mx), 0.0)
        m_ref[g] = mx
        l_ref[g] = jnp.sum(cw, axis=1, keepdims=True) + jnp.sum(ow, axis=1, keepdims=True)
        o_ref[:, g * HD : (g + 1) * HD] = jnp.dot(
            cw.astype(jnp.bfloat16), ctx_vals, preferred_element_type=jnp.float32
        ) + jnp.dot(ow.astype(jnp.bfloat16), own_vals, preferred_element_type=jnp.float32)


def attend(queries, ctx_blocks, own_keys, own_vals, ctx_bias, key_rank, group_size, score_scale):
    tokens, q_width = queries.shape
    slots, double_len, _ = ctx_blocks.shape
    block_len = double_len // 2
    ctx_count = slots * block_len
    own_count = own_keys.shape[0]
    heads = q_width // HD
    kvh = heads // group_size
    tq = min(tokens, 128)
    return pl.pallas_call(
        functools.partial(attn_kernel, score_scale=score_scale, group=group_size),
        grid=(tokens // tq, kvh),
        in_specs=[
            pl.BlockSpec((1, ctx_count), lambda i, h: (0, 0)),
            pl.BlockSpec((1, own_count), lambda i, h: (0, 0)),
            pl.BlockSpec((tq, HD * group_size), lambda i, h: (i, h)),
            pl.BlockSpec((slots, block_len, HD), lambda i, h: (0, 0, h)),
            pl.BlockSpec((own_count, HD), lambda i, h: (0, h)),
            pl.BlockSpec((slots, block_len, HD), lambda i, h: (0, 1, h)),
            pl.BlockSpec((own_count, HD), lambda i, h: (0, h)),
        ],
        out_specs=[
            pl.BlockSpec((tq, HD * group_size), lambda i, h: (i, h)),
            pl.BlockSpec((group_size, tq, 1), lambda i, h: (h, i, 0)),
            pl.BlockSpec((group_size, tq, 1), lambda i, h: (h, i, 0)),
        ],
        out_shape=[
            jax.ShapeDtypeStruct((tokens, q_width), jnp.float32),
            jax.ShapeDtypeStruct((heads, tokens, 1), jnp.float32),
            jax.ShapeDtypeStruct((heads, tokens, 1), jnp.float32),
        ],
    )(ctx_bias, key_rank, queries, ctx_blocks, own_keys, ctx_blocks, own_vals)


def shift_pairs(shards, step):
    chips = shards // 2
    return [(i, ((i // 2 + step) % chips) * 2 + i % 2) for i in range(shards)]


def core_pairs(shards):
    return [(i, i ^ 1) for i in range(shards)]


def pick_core(pair, core):
    return jnp.take(pair, jnp.arange(2) ^ core, axis=1)


def hier_reduce_gather(partials, shards, own_index):
    chips = shards // 2
    core = own_index % 2
    chip = own_index // 2
    tree = jax.tree.map

    def split(x):
        return x.reshape((chips, 2) + x.shape[1:])

    by_core = tree(split, partials)
    mine = tree(lambda x: lax.dynamic_index_in_dim(x, core, 1, keepdims=False), by_core)
    other = tree(lambda x: lax.dynamic_index_in_dim(x, 1 - core, 1, keepdims=False), by_core)
    chip_sum = tree(jnp.add, mine, lax.ppermute(other, "ctx", core_pairs(shards)))
    total = tree(lambda x: lax.dynamic_index_in_dim(x, chip, 0, keepdims=False), chip_sum)
    for step in range(1, chips):
        send = tree(
            lambda x: lax.dynamic_index_in_dim(x, (chip + step) % chips, 0, keepdims=False),
            chip_sum,
        )
        total = tree(jnp.add, total, lax.ppermute(send, "ctx", shift_pairs(shards, step)))
    rounded = tree(lambda x: x.astype(jnp.bfloat16), total)
    got = [rounded] + [
        lax.ppermute(rounded, "ctx", shift_pairs(shards, step)) for step in range(1, chips)
    ]
    order = (chip - jnp.arange(chips)) % chips
    by_chip = tree(lambda *xs: jnp.take(jnp.stack(xs), order, axis=0), *got)
    partner = lax.ppermute(by_chip, "ctx", core_pairs(shards))

    def join(x, y):
        pair = pick_core(jnp.stack([x, y], axis=1), core)
        return pair.reshape((shards,) + pair.shape[2:])

    return tree(join, by_chip, partner)


def merge(parts, sums_width):
    sums = [p[..., :sums_width] for p in parts]
    maxes = [p[..., sums_width:sums_width + (p.shape[-1] - sums_width) // 2] for p in parts]
    totals = [p[..., sums_width + (p.shape[-1] - sums_width) // 2:] for p in parts]
    best = maxes[0]
    for m in maxes[1:]:
        best = jnp.maximum(best, m)
    factors = [jnp.exp(m - best) for m in maxes]
    heads = best.shape[-1]
    lead = sums[0].shape[:-1]
    out_sum = sum(
        s.reshape(lead + (heads, HD)) * f[..., None] for s, f in zip(sums, factors)
    ).reshape(lead + (sums_width,))
    out_total = sum(t * f for t, f in zip(totals, factors))
    return jnp.concatenate([out_sum, best, out_total], axis=-1)


def hier_combine(sent, shards, own_index, sums_width):
    chips = shards // 2
    core = own_index % 2
    chip = own_index // 2
    by_core = sent.reshape((chips, 2) + sent.shape[1:])
    mine = lax.dynamic_index_in_dim(by_core, core, 1, keepdims=False)
    other = lax.dynamic_index_in_dim(by_core, 1 - core, 1, keepdims=False)
    chip_merged = merge([mine, lax.ppermute(other, "ctx", core_pairs(shards))], sums_width)
    parts = [lax.dynamic_index_in_dim(chip_merged, chip, 0, keepdims=False)]
    for step in range(1, chips):
        send = lax.dynamic_index_in_dim(chip_merged, (chip + step) % chips, 0, keepdims=False)
        parts.append(lax.ppermute(send, "ctx", shift_pairs(shards, step)))
    return merge(parts, sums_width)


def body(
    question_hidden,
    recomp_hidden,
    norm_gain,
    w_query,
    w_keyval,
    pool_codes,
    pool_scales,
    block_owner,
    block_slot,
    recomp_pos,
):
    shards = lax.axis_size("ctx")
    own_index = lax.axis_index("ctx")
    q_rows = question_hidden.shape[0]
    r_rows = recomp_hidden.shape[0]
    row_count = q_rows + r_rows
    kv_width = w_keyval.shape[2]
    kv_heads = kv_width // HD
    q_width = w_query.shape[1]
    heads = q_width // HD
    group_size = q_width // kv_width
    score_scale = HD ** (-0.5)

    owners = block_owner[:, 0].reshape(shards, -1)
    per_dev = owners.shape[1]
    slot_table = block_slot.reshape(shards, per_dev)
    capacity = max(2, 2 * per_dev // shards)
    positions = jnp.arange(per_dev)
    earlier_mask = positions[None, :] < positions[:, None]
    same_owner = owners[:, :, None] == owners[:, None, :]
    order_rank = jnp.sum((same_owner & earlier_mask[None]).astype(jnp.int32), axis=2)
    slot_ids = jnp.arange(capacity)
    chosen = (owners == own_index)[:, :, None] & (order_rank[:, :, None] == slot_ids[None, None, :])
    send_slot = jnp.sum(jnp.where(chosen, slot_table[:, :, None], 0), axis=1).reshape(-1)
    block_len = pool_codes.shape[2]
    send_codes = jnp.take(pool_codes, send_slot, axis=0)
    send_scales = jnp.take(pool_scales, send_slot, axis=0)
    send_blocks = (
        send_codes.astype(jnp.float32).reshape(shards * capacity, 2, block_len, kv_heads, HD)
        * send_scales.astype(jnp.float32)[:, :, None, :, None]
    ).astype(jnp.bfloat16).reshape((shards, capacity, 2, block_len, kv_width))
    send_blocks = lax.optimization_barrier(send_blocks)
    ctx_dev = per_dev * block_len
    slot_valid = jnp.any(chosen, axis=1)
    slot_block = jnp.sum(jnp.where(chosen, positions[None, :, None], 0), axis=1)
    slot_base = jnp.arange(shards)[:, None] * ctx_dev + slot_block * block_len
    slot_pos = jnp.where(
        slot_valid[:, :, None], slot_base[:, :, None] + jnp.arange(block_len), -1
    ).reshape(-1)

    normed = jnp.concatenate(
        [rms_rows(question_hidden, norm_gain), rms_rows(recomp_hidden, norm_gain)], axis=0
    )
    pieces = lax.all_to_all(normed, "ctx", split_axis=1, concat_axis=0, tiled=True)
    width_part = pieces.shape[1]
    arranged = pieces.reshape(shards, row_count, width_part)
    question_part = arranged[:, :q_rows, :].reshape(shards * q_rows, width_part)
    query_part = jnp.dot(question_part, w_query, preferred_element_type=jnp.float32)
    kv_part = jnp.einsum("tk,kcn->tcn", pieces, w_keyval, preferred_element_type=jnp.float32)

    every_query, every_kv = hier_reduce_gather(
        (
            query_part.reshape(shards, q_rows, q_width),
            kv_part.reshape(shards, row_count, 2, kv_width),
        ),
        shards,
        own_index,
    )
    send_later, every_query, every_kv = lax.optimization_barrier(
        (send_blocks, every_query, every_kv)
    )
    by_shift = [lax.dynamic_index_in_dim(send_later, own_index, 0, keepdims=False)]
    for step in range(1, shards):
        target = (own_index + step) % shards
        by_shift.append(
            lax.ppermute(
                lax.dynamic_index_in_dim(send_later, target, 0, keepdims=False),
                "ctx",
                [(i, (i + step) % shards) for i in range(shards)],
            )
        )
    got_blocks = jnp.stack(by_shift)
    every_query = every_query.reshape(shards * q_rows, q_width)
    own_kv = lax.dynamic_index_in_dim(every_kv, own_index, 0, keepdims=False)
    recomp_kv = every_kv[:, q_rows:].reshape(shards * r_rows, 2, kv_width)

    own_owner = lax.dynamic_index_in_dim(owners, own_index, 0, keepdims=False)
    own_rank = lax.dynamic_index_in_dim(order_rank, own_index, 0, keepdims=False)
    flat_index = ((own_index - own_owner) % shards) * capacity + own_rank
    local_pos = recomp_pos - own_index * ctx_dev
    match = local_pos[None, :] == jnp.arange(ctx_dev)[:, None]
    hit = jnp.any(match, axis=1)
    one_hot = match.astype(jnp.bfloat16)
    by_slot = got_blocks.reshape((shards * capacity, 2, block_len, kv_width))
    kv_parts = []
    for c in range(2):
        placed = jnp.dot(
            one_hot, recomp_kv[:, c], preferred_element_type=jnp.float32
        ).astype(jnp.bfloat16)
        cached = jnp.take(by_slot[:, c], flat_index, axis=0).reshape(ctx_dev, kv_width)
        kv_parts.append(jnp.where(hit[:, None], placed, cached))
    kv_cache = jnp.stack(kv_parts)

    replaced = jnp.any(recomp_pos[None, :] == slot_pos[:, None], axis=1)
    ctx_bias = jnp.where((slot_pos >= 0) & ~replaced, 0.0, neg_large).astype(jnp.float32)[None, :]
    own_row = jnp.arange(row_count)
    key_rank = jnp.where(own_row < q_rows, own_index * q_rows + own_row, -1).astype(jnp.int32)[None, :]

    part_sums, part_max, part_total = attend(
        every_query,
        send_blocks.reshape(shards * capacity, 2 * block_len, kv_width),
        own_kv[:, 0],
        own_kv[:, 1],
        ctx_bias,
        key_rank,
        group_size,
        score_scale,
    )

    def by_token(value):
        return jnp.transpose(value[:, :, 0]).reshape(shards, q_rows, heads)

    sent = jnp.concatenate(
        [part_sums.reshape(shards, q_rows, q_width), by_token(part_max), by_token(part_total)],
        axis=2,
    )
    got = hier_combine(sent, shards, own_index, q_width)
    weighted = got[:, :q_width].reshape(q_rows, heads, HD)
    row_total = got[:, q_width + heads :]
    attended = (weighted / row_total[..., None]).reshape(q_rows, q_width).astype(jnp.bfloat16)
    return (attended, kv_cache)


def solution(mesh):
    placed = (
        P(("groups", "ctx"), None),
        P(("groups", "ctx"), None),
        P(),
        P("ctx", "tp"),
        P("ctx", None, "tp"),
        P(("groups", "ctx"), None, None, "tp"),
        P(("groups", "ctx"), None, "tp"),
        P("groups", None),
        P("groups"),
        P("groups"),
    )
    return jax.shard_map(
        body,
        mesh=mesh,
        in_specs=placed,
        out_specs=(P(("groups", "ctx"), "tp"), P(None, ("groups", "ctx"), "tp")),
        check_vma=False,
    )
```

```python
import functools

import jax
import jax.numpy as jnp
from jax import lax
from jax.experimental import pallas as pl
from jax.sharding import PartitionSpec as P


HD = 128


norm_eps = 1e-05
neg_large = -1e30


def rms_rows(hidden, norm_gain):
    floats = hidden.astype(jnp.float32)
    factor = lax.rsqrt(jnp.mean(floats * floats, axis=-1, keepdims=True) + norm_eps)
    return (floats * factor * norm_gain.astype(jnp.float32)).astype(jnp.bfloat16)


def attn_kernel(bias_ref, rank_ref, q_ref, kc_ref, kq_ref, vc_ref, vq_ref, o_ref, m_ref, l_ref, *, score_scale, group):
    slots, block_len, width = kc_ref.shape
    ctx_keys = kc_ref[...].reshape(slots * block_len, width)
    ctx_vals = vc_ref[...].reshape(slots * block_len, width)
    own_keys = kq_ref[...]
    own_vals = vq_ref[...]
    bias = bias_ref[...]
    dims = (((1,), (1,)), ((), ()))
    tq = q_ref.shape[0]
    first = pl.program_id(0) * tq
    token = first + lax.broadcasted_iota(jnp.int32, (tq, own_keys.shape[0]), 0)
    shown = rank_ref[...] <= token
    for g in range(group):
        queries = q_ref[:, g * HD : (g + 1) * HD]
        cs = (
            lax.dot_general(queries, ctx_keys, dims, preferred_element_type=jnp.float32)
            * score_scale
            + bias
        )
        os_ = (
            lax.dot_general(queries, own_keys, dims, preferred_element_type=jnp.float32)
            * score_scale
        )
        om = jnp.where(shown, os_, neg_large)
        mx = jnp.maximum(jnp.max(cs, axis=1, keepdims=True), jnp.max(om, axis=1, keepdims=True))
        cw = jnp.exp(cs - mx)
        ow = jnp.where(shown, jnp.exp(om - mx), 0.0)
        m_ref[g] = mx
        l_ref[g] = jnp.sum(cw, axis=1, keepdims=True) + jnp.sum(ow, axis=1, keepdims=True)
        o_ref[:, g * HD : (g + 1) * HD] = jnp.dot(
            cw.astype(jnp.bfloat16), ctx_vals, preferred_element_type=jnp.float32
        ) + jnp.dot(ow.astype(jnp.bfloat16), own_vals, preferred_element_type=jnp.float32)


def attend(queries, ctx_blocks, own_keys, own_vals, ctx_bias, key_rank, group_size, score_scale):
    tokens, q_width = queries.shape
    slots, double_len, _ = ctx_blocks.shape
    block_len = double_len // 2
    ctx_count = slots * block_len
    own_count = own_keys.shape[0]
    heads = q_width // HD
    kvh = heads // group_size
    tq = min(tokens, 128)
    return pl.pallas_call(
        functools.partial(attn_kernel, score_scale=score_scale, group=group_size),
        grid=(tokens // tq, kvh),
        in_specs=[
            pl.BlockSpec((1, ctx_count), lambda i, h: (0, 0)),
            pl.BlockSpec((1, own_count), lambda i, h: (0, 0)),
            pl.BlockSpec((tq, HD * group_size), lambda i, h: (i, h)),
            pl.BlockSpec((slots, block_len, HD), lambda i, h: (0, 0, h)),
            pl.BlockSpec((own_count, HD), lambda i, h: (0, h)),
            pl.BlockSpec((slots, block_len, HD), lambda i, h: (0, 1, h)),
            pl.BlockSpec((own_count, HD), lambda i, h: (0, h)),
        ],
        out_specs=[
            pl.BlockSpec((tq, HD * group_size), lambda i, h: (i, h)),
            pl.BlockSpec((group_size, tq, 1), lambda i, h: (h, i, 0)),
            pl.BlockSpec((group_size, tq, 1), lambda i, h: (h, i, 0)),
        ],
        out_shape=[
            jax.ShapeDtypeStruct((tokens, q_width), jnp.float32),
            jax.ShapeDtypeStruct((heads, tokens, 1), jnp.float32),
            jax.ShapeDtypeStruct((heads, tokens, 1), jnp.float32),
        ],
    )(ctx_bias, key_rank, queries, ctx_blocks, own_keys, ctx_blocks, own_vals)


def shift_pairs(shards, step):
    chips = shards // 2
    return [(i, ((i // 2 + step) % chips) * 2 + i % 2) for i in range(shards)]


def core_pairs(shards):
    return [(i, i ^ 1) for i in range(shards)]


def pick_core(pair, core):
    return jnp.take(pair, jnp.arange(2) ^ core, axis=1)


def hier_reduce_gather(partials, shards, own_index):
    chips = shards // 2
    core = own_index % 2
    chip = own_index // 2
    tree = jax.tree.map

    def split(x):
        return x.reshape((chips, 2) + x.shape[1:])

    by_core = tree(split, partials)
    mine = tree(lambda x: lax.dynamic_index_in_dim(x, core, 1, keepdims=False), by_core)
    other = tree(lambda x: lax.dynamic_index_in_dim(x, 1 - core, 1, keepdims=False), by_core)
    chip_sum = tree(jnp.add, mine, lax.ppermute(other, "ctx", core_pairs(shards)))
    total = tree(lambda x: lax.dynamic_index_in_dim(x, chip, 0, keepdims=False), chip_sum)
    for step in range(1, chips):
        send = tree(
            lambda x: lax.dynamic_index_in_dim(x, (chip + step) % chips, 0, keepdims=False),
            chip_sum,
        )
        total = tree(jnp.add, total, lax.ppermute(send, "ctx", shift_pairs(shards, step)))
    rounded = tree(lambda x: x.astype(jnp.bfloat16), total)
    got = [rounded] + [
        lax.ppermute(rounded, "ctx", shift_pairs(shards, step)) for step in range(1, chips)
    ]
    order = (chip - jnp.arange(chips)) % chips
    by_chip = tree(lambda *xs: jnp.take(jnp.stack(xs), order, axis=0), *got)
    partner = lax.ppermute(by_chip, "ctx", core_pairs(shards))

    def join(x, y):
        pair = pick_core(jnp.stack([x, y], axis=1), core)
        return pair.reshape((shards,) + pair.shape[2:])

    return tree(join, by_chip, partner)


def merge(parts, sums_width):
    sums = [p[..., :sums_width] for p in parts]
    maxes = [p[..., sums_width:sums_width + (p.shape[-1] - sums_width) // 2] for p in parts]
    totals = [p[..., sums_width + (p.shape[-1] - sums_width) // 2:] for p in parts]
    best = maxes[0]
    for m in maxes[1:]:
        best = jnp.maximum(best, m)
    factors = [jnp.exp(m - best) for m in maxes]
    heads = best.shape[-1]
    lead = sums[0].shape[:-1]
    out_sum = sum(
        s.reshape(lead + (heads, HD)) * f[..., None] for s, f in zip(sums, factors)
    ).reshape(lead + (sums_width,))
    out_total = sum(t * f for t, f in zip(totals, factors))
    return jnp.concatenate([out_sum, best, out_total], axis=-1)


def hier_combine(sent, shards, own_index, sums_width):
    chips = shards // 2
    core = own_index % 2
    chip = own_index // 2
    by_core = sent.reshape((chips, 2) + sent.shape[1:])
    mine = lax.dynamic_index_in_dim(by_core, core, 1, keepdims=False)
    other = lax.dynamic_index_in_dim(by_core, 1 - core, 1, keepdims=False)
    chip_merged = merge([mine, lax.ppermute(other, "ctx", core_pairs(shards))], sums_width)
    parts = [lax.dynamic_index_in_dim(chip_merged, chip, 0, keepdims=False)]
    for step in range(1, chips):
        send = lax.dynamic_index_in_dim(chip_merged, (chip + step) % chips, 0, keepdims=False)
        parts.append(lax.ppermute(send, "ctx", shift_pairs(shards, step)))
    return merge(parts, sums_width)


def body(
    question_hidden,
    recomp_hidden,
    norm_gain,
    w_query,
    w_keyval,
    pool_codes,
    pool_scales,
    block_owner,
    block_slot,
    recomp_pos,
):
    shards = lax.axis_size("ctx")
    own_index = lax.axis_index("ctx")
    q_rows = question_hidden.shape[0]
    r_rows = recomp_hidden.shape[0]
    row_count = q_rows + r_rows
    kv_width = w_keyval.shape[2]
    kv_heads = kv_width // HD
    q_width = w_query.shape[1]
    heads = q_width // HD
    group_size = q_width // kv_width
    score_scale = HD ** (-0.5)

    owners = block_owner[:, 0].reshape(shards, -1)
    per_dev = owners.shape[1]
    slot_table = block_slot.reshape(shards, per_dev)
    capacity = max(2, 2 * per_dev // shards)
    positions = jnp.arange(per_dev)
    earlier_mask = positions[None, :] < positions[:, None]
    same_owner = owners[:, :, None] == owners[:, None, :]
    order_rank = jnp.sum((same_owner & earlier_mask[None]).astype(jnp.int32), axis=2)
    slot_ids = jnp.arange(capacity)
    chosen = (owners == own_index)[:, :, None] & (order_rank[:, :, None] == slot_ids[None, None, :])
    send_slot = jnp.sum(jnp.where(chosen, slot_table[:, :, None], 0), axis=1).reshape(-1)
    block_len = pool_codes.shape[2]
    send_codes = jnp.take(pool_codes, send_slot, axis=0)
    send_scales = jnp.take(pool_scales, send_slot, axis=0)
    send_blocks = (
        send_codes.astype(jnp.float32).reshape(shards * capacity, 2, block_len, kv_heads, HD)
        * send_scales.astype(jnp.float32)[:, :, None, :, None]
    ).astype(jnp.bfloat16).reshape((shards, capacity, 2, block_len, kv_width))
    send_blocks = lax.optimization_barrier(send_blocks)
    ctx_dev = per_dev * block_len
    slot_valid = jnp.any(chosen, axis=1)
    slot_block = jnp.sum(jnp.where(chosen, positions[None, :, None], 0), axis=1)
    slot_base = jnp.arange(shards)[:, None] * ctx_dev + slot_block * block_len
    slot_pos = jnp.where(
        slot_valid[:, :, None], slot_base[:, :, None] + jnp.arange(block_len), -1
    ).reshape(-1)

    normed = jnp.concatenate(
        [rms_rows(question_hidden, norm_gain), rms_rows(recomp_hidden, norm_gain)], axis=0
    )
    pieces = lax.all_to_all(normed, "ctx", split_axis=1, concat_axis=0, tiled=True)
    early_step = min(2, shards - 1)
    send_early, pieces = lax.optimization_barrier((send_blocks, pieces))
    early_blocks = lax.ppermute(
        lax.dynamic_index_in_dim(send_early, (own_index + early_step) % shards, 0, keepdims=False),
        "ctx",
        [(i, (i + early_step) % shards) for i in range(shards)],
    )
    width_part = pieces.shape[1]
    arranged = pieces.reshape(shards, row_count, width_part)
    question_part = arranged[:, :q_rows, :].reshape(shards * q_rows, width_part)
    query_part = jnp.dot(question_part, w_query, preferred_element_type=jnp.float32)
    kv_part = jnp.einsum("tk,kcn->tcn", pieces, w_keyval, preferred_element_type=jnp.float32)

    every_query, every_kv = hier_reduce_gather(
        (
            query_part.reshape(shards, q_rows, q_width),
            kv_part.reshape(shards, row_count, 2, kv_width),
        ),
        shards,
        own_index,
    )
    send_later, every_query, every_kv = lax.optimization_barrier(
        (send_blocks, every_query, every_kv)
    )
    by_shift = [lax.dynamic_index_in_dim(send_later, own_index, 0, keepdims=False)]
    for step in range(1, shards):
        if step == early_step:
            by_shift.append(early_blocks)
            continue
        target = (own_index + step) % shards
        by_shift.append(
            lax.ppermute(
                lax.dynamic_index_in_dim(send_later, target, 0, keepdims=False),
                "ctx",
                [(i, (i + step) % shards) for i in range(shards)],
            )
        )
    got_blocks = jnp.stack(by_shift)
    every_query = every_query.reshape(shards * q_rows, q_width)
    own_kv = lax.dynamic_index_in_dim(every_kv, own_index, 0, keepdims=False)
    recomp_kv = every_kv[:, q_rows:].reshape(shards * r_rows, 2, kv_width)

    own_owner = lax.dynamic_index_in_dim(owners, own_index, 0, keepdims=False)
    own_rank = lax.dynamic_index_in_dim(order_rank, own_index, 0, keepdims=False)
    flat_index = ((own_index - own_owner) % shards) * capacity + own_rank
    local_pos = recomp_pos - own_index * ctx_dev
    match = local_pos[None, :] == jnp.arange(ctx_dev)[:, None]
    hit = jnp.any(match, axis=1)
    one_hot = match.astype(jnp.bfloat16)
    by_slot = got_blocks.reshape((shards * capacity, 2, block_len, kv_width))
    kv_parts = []
    for c in range(2):
        placed = jnp.dot(
            one_hot, recomp_kv[:, c], preferred_element_type=jnp.float32
        ).astype(jnp.bfloat16)
        cached = jnp.take(by_slot[:, c], flat_index, axis=0).reshape(ctx_dev, kv_width)
        kv_parts.append(jnp.where(hit[:, None], placed, cached))
    kv_cache = jnp.stack(kv_parts)

    replaced = jnp.any(recomp_pos[None, :] == slot_pos[:, None], axis=1)
    ctx_bias = jnp.where((slot_pos >= 0) & ~replaced, 0.0, neg_large).astype(jnp.float32)[None, :]
    own_row = jnp.arange(row_count)
    key_rank = jnp.where(own_row < q_rows, own_index * q_rows + own_row, -1).astype(jnp.int32)[None, :]

    part_sums, part_max, part_total = attend(
        every_query,
        send_blocks.reshape(shards * capacity, 2 * block_len, kv_width),
        own_kv[:, 0],
        own_kv[:, 1],
        ctx_bias,
        key_rank,
        group_size,
        score_scale,
    )

    def by_token(value):
        return jnp.transpose(value[:, :, 0]).reshape(shards, q_rows, heads)

    sent = jnp.concatenate(
        [part_sums.reshape(shards, q_rows, q_width), by_token(part_max), by_token(part_total)],
        axis=2,
    )
    got = hier_combine(sent, shards, own_index, q_width)
    weighted = got[:, :q_width].reshape(q_rows, heads, HD)
    row_total = got[:, q_width + heads :]
    attended = (weighted / row_total[..., None]).reshape(q_rows, q_width).astype(jnp.bfloat16)
    return (attended, kv_cache)


def solution(mesh):
    placed = (
        P(("groups", "ctx"), None),
        P(("groups", "ctx"), None),
        P(),
        P("ctx", "tp"),
        P("ctx", None, "tp"),
        P(("groups", "ctx"), None, None, "tp"),
        P(("groups", "ctx"), None, "tp"),
        P("groups", None),
        P("groups"),
        P("groups"),
    )
    return jax.shard_map(
        body,
        mesh=mesh,
        in_specs=placed,
        out_specs=(P(("groups", "ctx"), "tp"), P(None, ("groups", "ctx"), "tp")),
        check_vma=False,
    )
```

```python
import functools

import jax
import jax.numpy as jnp
from jax import lax
from jax.experimental import pallas as pl
from jax.sharding import PartitionSpec as P


HD = 128


norm_eps = 1e-05
neg_large = -1e30


def rms_rows(hidden, norm_gain):
    floats = hidden.astype(jnp.float32)
    factor = lax.rsqrt(jnp.mean(floats * floats, axis=-1, keepdims=True) + norm_eps)
    return (floats * factor * norm_gain.astype(jnp.float32)).astype(jnp.bfloat16)


def attn_kernel(bias_ref, rank_ref, q_ref, kc_ref, kq_ref, vc_ref, vq_ref, o_ref, m_ref, l_ref, *, score_scale, group):
    slots, block_len, width = kc_ref.shape
    ctx_keys = kc_ref[...].reshape(slots * block_len, width)
    ctx_vals = vc_ref[...].reshape(slots * block_len, width)
    own_keys = kq_ref[...]
    own_vals = vq_ref[...]
    bias = bias_ref[...]
    dims = (((1,), (1,)), ((), ()))
    tq = q_ref.shape[0]
    first = pl.program_id(0) * tq
    token = first + lax.broadcasted_iota(jnp.int32, (tq, own_keys.shape[0]), 0)
    shown = rank_ref[...] <= token
    for g in range(group):
        queries = q_ref[:, g * HD : (g + 1) * HD]
        cs = (
            lax.dot_general(queries, ctx_keys, dims, preferred_element_type=jnp.float32)
            * score_scale
            + bias
        )
        os_ = (
            lax.dot_general(queries, own_keys, dims, preferred_element_type=jnp.float32)
            * score_scale
        )
        om = jnp.where(shown, os_, neg_large)
        mx = jnp.maximum(jnp.max(cs, axis=1, keepdims=True), jnp.max(om, axis=1, keepdims=True))
        cw = jnp.exp(cs - mx)
        ow = jnp.where(shown, jnp.exp(om - mx), 0.0)
        m_ref[g] = mx
        l_ref[g] = jnp.sum(cw, axis=1, keepdims=True) + jnp.sum(ow, axis=1, keepdims=True)
        o_ref[:, g * HD : (g + 1) * HD] = jnp.dot(
            cw.astype(jnp.bfloat16), ctx_vals, preferred_element_type=jnp.float32
        ) + jnp.dot(ow.astype(jnp.bfloat16), own_vals, preferred_element_type=jnp.float32)


def attend(queries, ctx_blocks, own_keys, own_vals, ctx_bias, key_rank, group_size, score_scale):
    tokens, q_width = queries.shape
    slots, double_len, _ = ctx_blocks.shape
    block_len = double_len // 2
    ctx_count = slots * block_len
    own_count = own_keys.shape[0]
    heads = q_width // HD
    kvh = heads // group_size
    tq = min(tokens, 128)
    return pl.pallas_call(
        functools.partial(attn_kernel, score_scale=score_scale, group=group_size),
        grid=(tokens // tq, kvh),
        in_specs=[
            pl.BlockSpec((1, ctx_count), lambda i, h: (0, 0)),
            pl.BlockSpec((1, own_count), lambda i, h: (0, 0)),
            pl.BlockSpec((tq, HD * group_size), lambda i, h: (i, h)),
            pl.BlockSpec((slots, block_len, HD), lambda i, h: (0, 0, h)),
            pl.BlockSpec((own_count, HD), lambda i, h: (0, h)),
            pl.BlockSpec((slots, block_len, HD), lambda i, h: (0, 1, h)),
            pl.BlockSpec((own_count, HD), lambda i, h: (0, h)),
        ],
        out_specs=[
            pl.BlockSpec((tq, HD * group_size), lambda i, h: (i, h)),
            pl.BlockSpec((group_size, tq, 1), lambda i, h: (h, i, 0)),
            pl.BlockSpec((group_size, tq, 1), lambda i, h: (h, i, 0)),
        ],
        out_shape=[
            jax.ShapeDtypeStruct((tokens, q_width), jnp.float32),
            jax.ShapeDtypeStruct((heads, tokens, 1), jnp.float32),
            jax.ShapeDtypeStruct((heads, tokens, 1), jnp.float32),
        ],
    )(ctx_bias, key_rank, queries, ctx_blocks, own_keys, ctx_blocks, own_vals)


def shift_pairs(shards, step):
    chips = shards // 2
    return [(i, ((i // 2 + step) % chips) * 2 + i % 2) for i in range(shards)]


def core_pairs(shards):
    return [(i, i ^ 1) for i in range(shards)]


def pick_core(pair, core):
    return jnp.take(pair, jnp.arange(2) ^ core, axis=1)


def hier_reduce_gather(partials, shards, own_index):
    chips = shards // 2
    core = own_index % 2
    chip = own_index // 2
    tree = jax.tree.map

    def split(x):
        return x.reshape((chips, 2) + x.shape[1:])

    by_core = tree(split, partials)
    mine = tree(lambda x: lax.dynamic_index_in_dim(x, core, 1, keepdims=False), by_core)
    other = tree(lambda x: lax.dynamic_index_in_dim(x, 1 - core, 1, keepdims=False), by_core)
    chip_sum = tree(jnp.add, mine, lax.ppermute(other, "ctx", core_pairs(shards)))
    total = tree(lambda x: lax.dynamic_index_in_dim(x, chip, 0, keepdims=False), chip_sum)
    for step in range(1, chips):
        send = tree(
            lambda x: lax.dynamic_index_in_dim(x, (chip + step) % chips, 0, keepdims=False),
            chip_sum,
        )
        total = tree(jnp.add, total, lax.ppermute(send, "ctx", shift_pairs(shards, step)))
    rounded = tree(lambda x: x.astype(jnp.bfloat16), total)
    got = [rounded] + [
        lax.ppermute(rounded, "ctx", shift_pairs(shards, step)) for step in range(1, chips)
    ]
    order = (chip - jnp.arange(chips)) % chips
    by_chip = tree(lambda *xs: jnp.take(jnp.stack(xs), order, axis=0), *got)
    partner = lax.ppermute(by_chip, "ctx", core_pairs(shards))

    def join(x, y):
        pair = pick_core(jnp.stack([x, y], axis=1), core)
        return pair.reshape((shards,) + pair.shape[2:])

    return tree(join, by_chip, partner)


def merge(parts, sums_width):
    sums = [p[..., :sums_width] for p in parts]
    maxes = [p[..., sums_width:sums_width + (p.shape[-1] - sums_width) // 2] for p in parts]
    totals = [p[..., sums_width + (p.shape[-1] - sums_width) // 2:] for p in parts]
    best = maxes[0]
    for m in maxes[1:]:
        best = jnp.maximum(best, m)
    factors = [jnp.exp(m - best) for m in maxes]
    heads = best.shape[-1]
    lead = sums[0].shape[:-1]
    out_sum = sum(
        s.reshape(lead + (heads, HD)) * f[..., None] for s, f in zip(sums, factors)
    ).reshape(lead + (sums_width,))
    out_total = sum(t * f for t, f in zip(totals, factors))
    return jnp.concatenate([out_sum, best, out_total], axis=-1)


def hier_combine(sent, shards, own_index, sums_width):
    chips = shards // 2
    core = own_index % 2
    chip = own_index // 2
    by_core = sent.reshape((chips, 2) + sent.shape[1:])
    mine = lax.dynamic_index_in_dim(by_core, core, 1, keepdims=False)
    other = lax.dynamic_index_in_dim(by_core, 1 - core, 1, keepdims=False)
    chip_merged = merge([mine, lax.ppermute(other, "ctx", core_pairs(shards))], sums_width)
    parts = [lax.dynamic_index_in_dim(chip_merged, chip, 0, keepdims=False)]
    heads = (sent.shape[-1] - sums_width) // 2
    for step in range(1, chips):
        send = lax.dynamic_index_in_dim(chip_merged, (chip + step) % chips, 0, keepdims=False)
        stats = send[..., sums_width:]
        totals = stats[..., heads:]
        lead = send.shape[:-1]
        normed = (
            send[..., :sums_width].reshape(lead + (heads, HD)) / totals[..., None]
        ).astype(jnp.bfloat16)
        got_normed, got_stats = lax.ppermute((normed, stats), "ctx", shift_pairs(shards, step))
        got_sums = (got_normed.astype(jnp.float32) * got_stats[..., heads:, None]).reshape(
            lead + (sums_width,)
        )
        parts.append(jnp.concatenate([got_sums, got_stats], axis=-1))
    return merge(parts, sums_width)


def body(
    question_hidden,
    recomp_hidden,
    norm_gain,
    w_query,
    w_keyval,
    pool_codes,
    pool_scales,
    block_owner,
    block_slot,
    recomp_pos,
):
    shards = lax.axis_size("ctx")
    own_index = lax.axis_index("ctx")
    q_rows = question_hidden.shape[0]
    r_rows = recomp_hidden.shape[0]
    row_count = q_rows + r_rows
    kv_width = w_keyval.shape[2]
    kv_heads = kv_width // HD
    q_width = w_query.shape[1]
    heads = q_width // HD
    group_size = q_width // kv_width
    score_scale = HD ** (-0.5)

    owners = block_owner[:, 0].reshape(shards, -1)
    per_dev = owners.shape[1]
    slot_table = block_slot.reshape(shards, per_dev)
    capacity = max(2, 2 * per_dev // shards)
    positions = jnp.arange(per_dev)
    earlier_mask = positions[None, :] < positions[:, None]
    same_owner = owners[:, :, None] == owners[:, None, :]
    order_rank = jnp.sum((same_owner & earlier_mask[None]).astype(jnp.int32), axis=2)
    slot_ids = jnp.arange(capacity)
    chosen = (owners == own_index)[:, :, None] & (order_rank[:, :, None] == slot_ids[None, None, :])
    send_slot = jnp.sum(jnp.where(chosen, slot_table[:, :, None], 0), axis=1).reshape(-1)
    block_len = pool_codes.shape[2]
    send_codes = jnp.take(pool_codes, send_slot, axis=0)
    send_scales = jnp.take(pool_scales, send_slot, axis=0)
    send_blocks = (
        send_codes.astype(jnp.float32).reshape(shards * capacity, 2, block_len, kv_heads, HD)
        * send_scales.astype(jnp.float32)[:, :, None, :, None]
    ).astype(jnp.bfloat16).reshape((shards, capacity, 2, block_len, kv_width))
    send_blocks = lax.optimization_barrier(send_blocks)
    ctx_dev = per_dev * block_len
    slot_valid = jnp.any(chosen, axis=1)
    slot_block = jnp.sum(jnp.where(chosen, positions[None, :, None], 0), axis=1)
    slot_base = jnp.arange(shards)[:, None] * ctx_dev + slot_block * block_len
    slot_pos = jnp.where(
        slot_valid[:, :, None], slot_base[:, :, None] + jnp.arange(block_len), -1
    ).reshape(-1)

    normed = jnp.concatenate(
        [rms_rows(question_hidden, norm_gain), rms_rows(recomp_hidden, norm_gain)], axis=0
    )
    pieces = lax.all_to_all(normed, "ctx", split_axis=1, concat_axis=0, tiled=True)
    width_part = pieces.shape[1]
    arranged = pieces.reshape(shards, row_count, width_part)
    question_part = arranged[:, :q_rows, :].reshape(shards * q_rows, width_part)
    query_part = jnp.dot(question_part, w_query, preferred_element_type=jnp.float32)
    kv_part = jnp.einsum("tk,kcn->tcn", pieces, w_keyval, preferred_element_type=jnp.float32)

    every_query, every_kv = hier_reduce_gather(
        (
            query_part.reshape(shards, q_rows, q_width),
            kv_part.reshape(shards, row_count, 2, kv_width),
        ),
        shards,
        own_index,
    )
    send_later, every_query, every_kv = lax.optimization_barrier(
        (send_blocks, every_query, every_kv)
    )
    by_shift = [lax.dynamic_index_in_dim(send_later, own_index, 0, keepdims=False)]
    for step in range(1, shards):
        target = (own_index + step) % shards
        by_shift.append(
            lax.ppermute(
                lax.dynamic_index_in_dim(send_later, target, 0, keepdims=False),
                "ctx",
                [(i, (i + step) % shards) for i in range(shards)],
            )
        )
    got_blocks = jnp.stack(by_shift)
    every_query = every_query.reshape(shards * q_rows, q_width)
    own_kv = lax.dynamic_index_in_dim(every_kv, own_index, 0, keepdims=False)
    recomp_kv = every_kv[:, q_rows:].reshape(shards * r_rows, 2, kv_width)

    own_owner = lax.dynamic_index_in_dim(owners, own_index, 0, keepdims=False)
    own_rank = lax.dynamic_index_in_dim(order_rank, own_index, 0, keepdims=False)
    flat_index = ((own_index - own_owner) % shards) * capacity + own_rank
    local_pos = recomp_pos - own_index * ctx_dev
    match = local_pos[None, :] == jnp.arange(ctx_dev)[:, None]
    hit = jnp.any(match, axis=1)
    one_hot = match.astype(jnp.bfloat16)
    by_slot = got_blocks.reshape((shards * capacity, 2, block_len, kv_width))
    kv_parts = []
    for c in range(2):
        placed = jnp.dot(
            one_hot, recomp_kv[:, c], preferred_element_type=jnp.float32
        ).astype(jnp.bfloat16)
        cached = jnp.take(by_slot[:, c], flat_index, axis=0).reshape(ctx_dev, kv_width)
        kv_parts.append(jnp.where(hit[:, None], placed, cached))
    kv_cache = jnp.stack(kv_parts)

    replaced = jnp.any(recomp_pos[None, :] == slot_pos[:, None], axis=1)
    ctx_bias = jnp.where((slot_pos >= 0) & ~replaced, 0.0, neg_large).astype(jnp.float32)[None, :]
    own_row = jnp.arange(row_count)
    key_rank = jnp.where(own_row < q_rows, own_index * q_rows + own_row, -1).astype(jnp.int32)[None, :]

    part_sums, part_max, part_total = attend(
        every_query,
        send_blocks.reshape(shards * capacity, 2 * block_len, kv_width),
        own_kv[:, 0],
        own_kv[:, 1],
        ctx_bias,
        key_rank,
        group_size,
        score_scale,
    )

    def by_token(value):
        return jnp.transpose(value[:, :, 0]).reshape(shards, q_rows, heads)

    sent = jnp.concatenate(
        [part_sums.reshape(shards, q_rows, q_width), by_token(part_max), by_token(part_total)],
        axis=2,
    )
    got = hier_combine(sent, shards, own_index, q_width)
    weighted = got[:, :q_width].reshape(q_rows, heads, HD)
    row_total = got[:, q_width + heads :]
    attended = (weighted / row_total[..., None]).reshape(q_rows, q_width).astype(jnp.bfloat16)
    return (attended, kv_cache)


def solution(mesh):
    placed = (
        P(("groups", "ctx"), None),
        P(("groups", "ctx"), None),
        P(),
        P("ctx", "tp"),
        P("ctx", None, "tp"),
        P(("groups", "ctx"), None, None, "tp"),
        P(("groups", "ctx"), None, "tp"),
        P("groups", None),
        P("groups"),
        P("groups"),
    )
    return jax.shard_map(
        body,
        mesh=mesh,
        in_specs=placed,
        out_specs=(P(("groups", "ctx"), "tp"), P(None, ("groups", "ctx"), "tp")),
        check_vma=False,
    )
```

```python
import functools

import jax
import jax.numpy as jnp
from jax import lax
from jax.experimental import pallas as pl
from jax.sharding import PartitionSpec as P


HD = 128


norm_eps = 1e-05
neg_large = -1e30


def rms_rows(hidden, norm_gain):
    floats = hidden.astype(jnp.float32)
    factor = lax.rsqrt(jnp.mean(floats * floats, axis=-1, keepdims=True) + norm_eps)
    return (floats * factor * norm_gain.astype(jnp.float32)).astype(jnp.bfloat16)


def attn_kernel(bias_ref, rank_ref, q_ref, kc_ref, kq_ref, vc_ref, vq_ref, o_ref, m_ref, l_ref, *, score_scale, group):
    slots, block_len, width = kc_ref.shape
    ctx_keys = kc_ref[...].reshape(slots * block_len, width)
    ctx_vals = vc_ref[...].reshape(slots * block_len, width)
    own_keys = kq_ref[...]
    own_vals = vq_ref[...]
    bias = bias_ref[...]
    dims = (((1,), (1,)), ((), ()))
    tq = q_ref.shape[0]
    first = pl.program_id(0) * tq
    token = first + lax.broadcasted_iota(jnp.int32, (tq, own_keys.shape[0]), 0)
    shown = rank_ref[...] <= token
    for g in range(group):
        queries = q_ref[:, g * HD : (g + 1) * HD]
        cs = (
            lax.dot_general(queries, ctx_keys, dims, preferred_element_type=jnp.float32)
            * score_scale
            + bias
        )
        os_ = (
            lax.dot_general(queries, own_keys, dims, preferred_element_type=jnp.float32)
            * score_scale
        )
        om = jnp.where(shown, os_, neg_large)
        mx = jnp.maximum(jnp.max(cs, axis=1, keepdims=True), jnp.max(om, axis=1, keepdims=True))
        cw = jnp.exp(cs - mx)
        ow = jnp.where(shown, jnp.exp(om - mx), 0.0)
        m_ref[g] = mx
        l_ref[g] = jnp.sum(cw, axis=1, keepdims=True) + jnp.sum(ow, axis=1, keepdims=True)
        o_ref[:, g * HD : (g + 1) * HD] = jnp.dot(
            cw.astype(jnp.bfloat16), ctx_vals, preferred_element_type=jnp.float32
        ) + jnp.dot(ow.astype(jnp.bfloat16), own_vals, preferred_element_type=jnp.float32)


def attend(queries, ctx_blocks, own_keys, own_vals, ctx_bias, key_rank, group_size, score_scale):
    tokens, q_width = queries.shape
    slots, double_len, _ = ctx_blocks.shape
    block_len = double_len // 2
    ctx_count = slots * block_len
    own_count = own_keys.shape[0]
    heads = q_width // HD
    kvh = heads // group_size
    tq = min(tokens, 128)
    return pl.pallas_call(
        functools.partial(attn_kernel, score_scale=score_scale, group=group_size),
        grid=(tokens // tq, kvh),
        in_specs=[
            pl.BlockSpec((1, ctx_count), lambda i, h: (0, 0)),
            pl.BlockSpec((1, own_count), lambda i, h: (0, 0)),
            pl.BlockSpec((tq, HD * group_size), lambda i, h: (i, h)),
            pl.BlockSpec((slots, block_len, HD), lambda i, h: (0, 0, h)),
            pl.BlockSpec((own_count, HD), lambda i, h: (0, h)),
            pl.BlockSpec((slots, block_len, HD), lambda i, h: (0, 1, h)),
            pl.BlockSpec((own_count, HD), lambda i, h: (0, h)),
        ],
        out_specs=[
            pl.BlockSpec((tq, HD * group_size), lambda i, h: (i, h)),
            pl.BlockSpec((group_size, tq, 1), lambda i, h: (h, i, 0)),
            pl.BlockSpec((group_size, tq, 1), lambda i, h: (h, i, 0)),
        ],
        out_shape=[
            jax.ShapeDtypeStruct((tokens, q_width), jnp.float32),
            jax.ShapeDtypeStruct((heads, tokens, 1), jnp.float32),
            jax.ShapeDtypeStruct((heads, tokens, 1), jnp.float32),
        ],
    )(ctx_bias, key_rank, queries, ctx_blocks, own_keys, ctx_blocks, own_vals)


def shift_pairs(shards, step):
    chips = shards // 2
    return [(i, ((i // 2 + step) % chips) * 2 + i % 2) for i in range(shards)]


def core_pairs(shards):
    return [(i, i ^ 1) for i in range(shards)]


def pick_core(pair, core):
    return jnp.take(pair, jnp.arange(2) ^ core, axis=1)


def hier_reduce_gather(partials, shards, own_index):
    chips = shards // 2
    core = own_index % 2
    chip = own_index // 2
    tree = jax.tree.map

    def split(x):
        return x.reshape((chips, 2) + x.shape[1:])

    by_core = tree(split, partials)
    mine = tree(lambda x: lax.dynamic_index_in_dim(x, core, 1, keepdims=False), by_core)
    other = tree(lambda x: lax.dynamic_index_in_dim(x, 1 - core, 1, keepdims=False), by_core)
    chip_sum = tree(jnp.add, mine, lax.ppermute(other, "ctx", core_pairs(shards)))
    total = tree(lambda x: lax.dynamic_index_in_dim(x, chip, 0, keepdims=False), chip_sum)
    for step in range(1, chips):
        send = tree(
            lambda x: lax.dynamic_index_in_dim(x, (chip + step) % chips, 0, keepdims=False),
            chip_sum,
        )
        total = tree(jnp.add, total, lax.ppermute(send, "ctx", shift_pairs(shards, step)))
    rounded = tree(lambda x: x.astype(jnp.bfloat16), total)
    got = [rounded] + [
        lax.ppermute(rounded, "ctx", shift_pairs(shards, step)) for step in range(1, chips)
    ]
    order = (chip - jnp.arange(chips)) % chips
    by_chip = tree(lambda *xs: jnp.take(jnp.stack(xs), order, axis=0), *got)
    partner = lax.ppermute(by_chip, "ctx", core_pairs(shards))

    def join(x, y):
        pair = pick_core(jnp.stack([x, y], axis=1), core)
        return pair.reshape((shards,) + pair.shape[2:])

    return tree(join, by_chip, partner)


def merge(parts, sums_width):
    sums = [p[..., :sums_width] for p in parts]
    maxes = [p[..., sums_width:sums_width + (p.shape[-1] - sums_width) // 2] for p in parts]
    totals = [p[..., sums_width + (p.shape[-1] - sums_width) // 2:] for p in parts]
    best = maxes[0]
    for m in maxes[1:]:
        best = jnp.maximum(best, m)
    factors = [jnp.exp(m - best) for m in maxes]
    heads = best.shape[-1]
    lead = sums[0].shape[:-1]
    out_sum = sum(
        s.reshape(lead + (heads, HD)) * f[..., None] for s, f in zip(sums, factors)
    ).reshape(lead + (sums_width,))
    out_total = sum(t * f for t, f in zip(totals, factors))
    return jnp.concatenate([out_sum, best, out_total], axis=-1)


def hier_combine(sent, shards, own_index, sums_width):
    chips = shards // 2
    core = own_index % 2
    chip = own_index // 2
    by_core = sent.reshape((chips, 2) + sent.shape[1:])
    mine = lax.dynamic_index_in_dim(by_core, core, 1, keepdims=False)
    other = lax.dynamic_index_in_dim(by_core, 1 - core, 1, keepdims=False)
    chip_merged = merge([mine, lax.ppermute(other, "ctx", core_pairs(shards))], sums_width)
    parts = [lax.dynamic_index_in_dim(chip_merged, chip, 0, keepdims=False)]
    heads = (sent.shape[-1] - sums_width) // 2
    for step in range(1, chips):
        send = lax.dynamic_index_in_dim(chip_merged, (chip + step) % chips, 0, keepdims=False)
        stats = send[..., sums_width:]
        totals = stats[..., heads:]
        lead = send.shape[:-1]
        normed = (
            send[..., :sums_width].reshape(lead + (heads, HD)) / totals[..., None]
        ).astype(jnp.bfloat16)
        got_normed, got_stats = lax.ppermute((normed, stats), "ctx", shift_pairs(shards, step))
        got_sums = (got_normed.astype(jnp.float32) * got_stats[..., heads:, None]).reshape(
            lead + (sums_width,)
        )
        parts.append(jnp.concatenate([got_sums, got_stats], axis=-1))
    return merge(parts, sums_width)


def body(
    question_hidden,
    recomp_hidden,
    norm_gain,
    w_query,
    w_keyval,
    pool_codes,
    pool_scales,
    block_owner,
    block_slot,
    recomp_pos,
):
    shards = lax.axis_size("ctx")
    own_index = lax.axis_index("ctx")
    q_rows = question_hidden.shape[0]
    r_rows = recomp_hidden.shape[0]
    row_count = q_rows + r_rows
    kv_width = w_keyval.shape[2]
    kv_heads = kv_width // HD
    q_width = w_query.shape[1]
    heads = q_width // HD
    group_size = q_width // kv_width
    score_scale = HD ** (-0.5)

    owners = block_owner[:, 0].reshape(shards, -1)
    per_dev = owners.shape[1]
    slot_table = block_slot.reshape(shards, per_dev)
    capacity = max(2, 2 * per_dev // shards)
    positions = jnp.arange(per_dev)
    earlier_mask = positions[None, :] < positions[:, None]
    same_owner = owners[:, :, None] == owners[:, None, :]
    order_rank = jnp.sum((same_owner & earlier_mask[None]).astype(jnp.int32), axis=2)
    slot_ids = jnp.arange(capacity)
    chosen = (owners == own_index)[:, :, None] & (order_rank[:, :, None] == slot_ids[None, None, :])
    send_slot = jnp.sum(jnp.where(chosen, slot_table[:, :, None], 0), axis=1).reshape(-1)
    block_len = pool_codes.shape[2]
    send_codes = jnp.take(pool_codes, send_slot, axis=0)
    send_scales = jnp.take(pool_scales, send_slot, axis=0)
    send_blocks = (
        send_codes.astype(jnp.float32).reshape(shards * capacity, 2, block_len, kv_heads, HD)
        * send_scales.astype(jnp.float32)[:, :, None, :, None]
    ).astype(jnp.bfloat16).reshape((shards, capacity, 2, block_len, kv_width))
    send_blocks = lax.optimization_barrier(send_blocks)
    ctx_dev = per_dev * block_len
    slot_valid = jnp.any(chosen, axis=1)
    slot_block = jnp.sum(jnp.where(chosen, positions[None, :, None], 0), axis=1)
    slot_base = jnp.arange(shards)[:, None] * ctx_dev + slot_block * block_len
    slot_pos = jnp.where(
        slot_valid[:, :, None], slot_base[:, :, None] + jnp.arange(block_len), -1
    ).reshape(-1)

    normed = jnp.concatenate(
        [rms_rows(question_hidden, norm_gain), rms_rows(recomp_hidden, norm_gain)], axis=0
    )
    width_share = normed.shape[1] // shards
    from_shift = [lax.dynamic_slice_in_dim(normed, own_index * width_share, width_share, 1)]
    for step in range(1, shards):
        target = (own_index + step) % shards
        from_shift.append(
            lax.ppermute(
                lax.dynamic_slice_in_dim(normed, target * width_share, width_share, 1),
                "ctx",
                [(i, (i + step) % shards) for i in range(shards)],
            )
        )
    pieces = jnp.take(
        jnp.stack(from_shift), (own_index - jnp.arange(shards)) % shards, axis=0
    ).reshape(shards * row_count, width_share)
    width_part = pieces.shape[1]
    arranged = pieces.reshape(shards, row_count, width_part)
    question_part = arranged[:, :q_rows, :].reshape(shards * q_rows, width_part)
    query_part = jnp.dot(question_part, w_query, preferred_element_type=jnp.float32)
    kv_part = jnp.einsum("tk,kcn->tcn", pieces, w_keyval, preferred_element_type=jnp.float32)

    every_query, every_kv = hier_reduce_gather(
        (
            query_part.reshape(shards, q_rows, q_width),
            kv_part.reshape(shards, row_count, 2, kv_width),
        ),
        shards,
        own_index,
    )
    send_later, every_query, every_kv = lax.optimization_barrier(
        (send_blocks, every_query, every_kv)
    )
    by_shift = [lax.dynamic_index_in_dim(send_later, own_index, 0, keepdims=False)]
    for step in range(1, shards):
        target = (own_index + step) % shards
        by_shift.append(
            lax.ppermute(
                lax.dynamic_index_in_dim(send_later, target, 0, keepdims=False),
                "ctx",
                [(i, (i + step) % shards) for i in range(shards)],
            )
        )
    got_blocks = jnp.stack(by_shift)
    every_query = every_query.reshape(shards * q_rows, q_width)
    own_kv = lax.dynamic_index_in_dim(every_kv, own_index, 0, keepdims=False)
    recomp_kv = every_kv[:, q_rows:].reshape(shards * r_rows, 2, kv_width)

    own_owner = lax.dynamic_index_in_dim(owners, own_index, 0, keepdims=False)
    own_rank = lax.dynamic_index_in_dim(order_rank, own_index, 0, keepdims=False)
    flat_index = ((own_index - own_owner) % shards) * capacity + own_rank
    local_pos = recomp_pos - own_index * ctx_dev
    match = local_pos[None, :] == jnp.arange(ctx_dev)[:, None]
    hit = jnp.any(match, axis=1)
    one_hot = match.astype(jnp.bfloat16)
    by_slot = got_blocks.reshape((shards * capacity, 2, block_len, kv_width))
    kv_parts = []
    for c in range(2):
        placed = jnp.dot(
            one_hot, recomp_kv[:, c], preferred_element_type=jnp.float32
        ).astype(jnp.bfloat16)
        cached = jnp.take(by_slot[:, c], flat_index, axis=0).reshape(ctx_dev, kv_width)
        kv_parts.append(jnp.where(hit[:, None], placed, cached))
    kv_cache = jnp.stack(kv_parts)

    replaced = jnp.any(recomp_pos[None, :] == slot_pos[:, None], axis=1)
    ctx_bias = jnp.where((slot_pos >= 0) & ~replaced, 0.0, neg_large).astype(jnp.float32)[None, :]
    own_row = jnp.arange(row_count)
    key_rank = jnp.where(own_row < q_rows, own_index * q_rows + own_row, -1).astype(jnp.int32)[None, :]

    part_sums, part_max, part_total = attend(
        every_query,
        send_blocks.reshape(shards * capacity, 2 * block_len, kv_width),
        own_kv[:, 0],
        own_kv[:, 1],
        ctx_bias,
        key_rank,
        group_size,
        score_scale,
    )

    def by_token(value):
        return jnp.transpose(value[:, :, 0]).reshape(shards, q_rows, heads)

    sent = jnp.concatenate(
        [part_sums.reshape(shards, q_rows, q_width), by_token(part_max), by_token(part_total)],
        axis=2,
    )
    got = hier_combine(sent, shards, own_index, q_width)
    weighted = got[:, :q_width].reshape(q_rows, heads, HD)
    row_total = got[:, q_width + heads :]
    attended = (weighted / row_total[..., None]).reshape(q_rows, q_width).astype(jnp.bfloat16)
    return (attended, kv_cache)


def solution(mesh):
    placed = (
        P(("groups", "ctx"), None),
        P(("groups", "ctx"), None),
        P(),
        P("ctx", "tp"),
        P("ctx", None, "tp"),
        P(("groups", "ctx"), None, None, "tp"),
        P(("groups", "ctx"), None, "tp"),
        P("groups", None),
        P("groups"),
        P("groups"),
    )
    return jax.shard_map(
        body,
        mesh=mesh,
        in_specs=placed,
        out_specs=(P(("groups", "ctx"), "tp"), P(None, ("groups", "ctx"), "tp")),
        check_vma=False,
    )
```
